512 devices in a mesh: cand: 8 (over y, core), doc: 64 (over z, x).
Axes of the slice: x: 4, y: 4, z: 16, core: 2. Of those that a mesh axis runs over, the one named last changes fastest.
Arguments:
- queries: bfloat16 [8192, 8192], P('doc'), may hold values from -6 to 50
- keys_values: bfloat16 [2, 8192, 1024], P(None, 'doc', 'cand'), may hold values from -6 to 50
- factors: float32 [8, 64], P('cand'), may hold values from 1 to 16
- lengths: int32 [16], replicated, may hold values from 1 to 1024, 8192 in all
Outputs:
- attended: bfloat16 [8, 8192, 8192], P('cand', 'doc')
The draws below stay inside these ranges and needn't reach their ends.
All inputs are finite; a program needn't handle non-finite values.
Results may differ from the reference program's by a relative error of at most 0.0053.
Values may be sent and summed in bfloat16 or wider, within the bound.
No kernel may reach another device: no remote copies, remote signals or barrier semaphores. Data moves between devices by JAX's collectives and lax.ppermute only.
A program may use at most 64 MiB of HBM per device.

```python
import math
import jax
import jax.numpy as jnp
import numpy as np
from jax import lax

H = 64
KVH = 8
HD = 128
TOK_DEV = 128
SPAN = 8
MAXLEN = 1024
TOKENS = 8192
DOCS = 16
CANDS = 8
N_DOC = 64


def draw_queries(key, part):
    full_shape = (TOKENS, H * HD)
    values = jnp.clip(jax.random.normal(key, full_shape, jnp.float32), -6.0, 6.0)
    return values.astype(jnp.bfloat16)


def draw_keys_values(key, part):
    full_shape = (TOKENS, KVH * HD)
    key_part, value_part = jax.random.split(key)
    values_rows = jnp.clip(jax.random.normal(value_part, full_shape, jnp.float32), -6.0, 6.0)
    keys_rows = jnp.clip(jax.random.normal(key_part, full_shape, jnp.float32), -6.0, 6.0)
    return jnp.stack([keys_rows, values_rows]).astype(jnp.bfloat16)


def levels(key, shape, cuts, smallest, top_value):
    loudness, own = 1.0, jax.random.fold_in(key, 6)
    for position, parts in cuts:
        heights = jnp.exp(jax.random.uniform(jax.random.fold_in(own, position), (parts,), jnp.float32, smallest / len(cuts), top_value / len(cuts)))
        loudness = loudness * jnp.repeat(heights, shape[position] // parts).reshape([-1 if axis == position else 1 for axis in range(len(shape))])
    return loudness


def profile(amount, total, most, skew):
    weights = [(1 << 20) // math.isqrt(standing ** skew) + 1 for standing in range(2, amount + 1)]
    rest, given = total - most - (amount - 1), [1] * (amount - 1)
    while rest > 0:
        free = [i for i in range(amount - 1) if given[i] < most]
        pool, left = sum([weights[i] for i in free]), rest
        for i in free:
            more = min(most - given[i], max(1, left * weights[i] // pool), rest)
            given[i] = given[i] + more
            rest = rest - more
    return np.array([most] + given)


def uneven_parts(rng, number_of, total, reach, skew):
    if number_of == 2:
        one = jax.random.randint(rng, (), max(1, total - reach), min(reach, total - 1) + 1)
        return jnp.stack([one, total - one])
    sizes = jnp.asarray(profile(number_of, total, reach, skew), jnp.int32)
    twos = (number_of - 1) // 2
    donor, sink = sizes[1:1 + 2 * twos:2], sizes[2:2 + 2 * twos:2]
    room = jnp.minimum(donor - 1, reach - sink)
    shifted = jax.random.randint(jax.random.fold_in(rng, 1), (twos,), 0, 1 << 20) % (room + 1)
    sizes = sizes.at[1:1 + 2 * twos:2].set(donor - shifted).at[2:2 + 2 * twos:2].set(sink + shifted)
    return sizes[jax.random.permutation(jax.random.fold_in(rng, 2), number_of)]


def setup_inputs(seed: int = 0) -> dict:
    arg_keys = jax.random.split(jax.random.key(seed), 5)
    queries = draw_queries(jax.random.fold_in(arg_keys[4], 71), 0)
    keys_values = draw_keys_values(jax.random.fold_in(arg_keys[4], 71), 0)
    factors = jnp.clip(jnp.exp(math.log(16.0) - 2.7725887 * jax.random.uniform(arg_keys[2], (CANDS, HD // 2), jnp.float32) ** levels(arg_keys[2], (CANDS, HD // 2), ((0, 8),), -0.2, 0.2)), 1.0, 16.0)
    lengths = uneven_parts(arg_keys[3], DOCS, TOKENS, MAXLEN, 2).astype(jnp.int32)
    return {"queries": queries, "keys_values": keys_values, "factors": factors, "lengths": lengths}


ROPE_BASE = 500000.0

def locate(index_rows, lengths):
    ends = jnp.cumsum(lengths).astype(jnp.int32)
    starts = (ends - lengths).astype(jnp.int32)
    docid = lax.optimization_barrier(jnp.sum((index_rows[:, None] >= ends[None, :]).astype(jnp.int32), axis=1)).astype(jnp.int32)
    onehot = docid[:, None] == jnp.arange(lengths.shape[0], dtype=jnp.int32)[None, :]
    first_row = lax.optimization_barrier(jnp.sum(jnp.where(onehot, starts[None, :], 0), axis=1)).astype(jnp.int32)
    valid = index_rows >= 0
    return (jnp.where(valid, docid, -1).astype(jnp.int32), jnp.where(valid, index_rows - first_row, 0).astype(jnp.int32))

def rotate(values, offsets, factor):
    row_count = values.shape[0]
    heads_here = values.shape[1] // HD
    half_dim = HD // 2
    shaped = values.reshape(row_count, heads_here, HD).astype(jnp.float32)
    inverse = jnp.power(ROPE_BASE, -2.0 * jnp.arange(half_dim, dtype=jnp.float32) / HD) / factor
    angles = offsets.astype(jnp.float32)[:, None] * inverse[None, :]
    cosine = jnp.cos(angles)[:, None, :]
    sine = jnp.sin(angles)[:, None, :]
    first_half = shaped[..., :half_dim]
    second_half = shaped[..., half_dim:]
    turned = jnp.concatenate([first_half * cosine - second_half * sine, second_half * cosine + first_half * sine], axis=-1)
    return turned.reshape(row_count, heads_here * HD).astype(jnp.bfloat16)

def attend(query_rot, key_rot, value_rows, query_doc, query_index, key_doc, key_index):
    row_count = query_rot.shape[0]
    key_count = key_rot.shape[0]
    group_size = H // KVH
    q_grouped = query_rot.reshape(row_count, KVH, group_size, HD).transpose(1, 0, 2, 3)
    k_grouped = key_rot.reshape(key_count, KVH, HD).transpose(1, 0, 2)
    v_grouped = value_rows.reshape(key_count, KVH, HD).transpose(1, 0, 2)
    allowed = (key_doc[None, :] == query_doc[:, None]) & (key_index[None, :] <= query_index[:, None]) & (key_doc[None, :] >= 0)
    scale = 1.0 / math.sqrt(HD)

    def per_group(operands):
        q_part, k_part, v_part = operands
        scores = jnp.einsum('rgd,wd->rgw', q_part.astype(jnp.float32), k_part.astype(jnp.float32)) * scale
        scores = jnp.where(allowed[:, None, :], scores, -1e+30)
        largest = lax.optimization_barrier(jnp.max(scores, axis=-1, keepdims=True))
        expw = jnp.exp(scores - largest)
        total = lax.optimization_barrier(jnp.sum(expw, axis=-1, keepdims=True))
        weights = expw.astype(jnp.bfloat16)
        numer = jnp.einsum('rgw,wd->rgd', weights.astype(jnp.float32), v_part.astype(jnp.float32))
        return (numer / total).astype(jnp.bfloat16)
    mixed = lax.map(per_group, (q_grouped, k_grouped, v_grouped))
    return mixed.transpose(1, 0, 2, 3).reshape(row_count, H * HD)

def reference(queries, keys_values, factors, lengths):
    margin = SPAN * TOK_DEV
    token_index = jnp.arange(TOKENS, dtype=jnp.int32)
    query_doc, query_offset = locate(token_index, lengths)
    padded_index = jnp.arange(-margin, TOKENS, dtype=jnp.int32)
    key_doc, key_offset = locate(padded_index, lengths)
    filler = jnp.zeros((margin, KVH * HD), jnp.bfloat16)
    value_padded = jnp.concatenate([filler, keys_values[1]], axis=0)

    def per_candidate(factor):
        query_rot = rotate(queries, query_offset, factor)
        key_rot = jnp.concatenate([filler, rotate(keys_values[0], key_offset[margin:], factor)], axis=0)

        def per_block(block):
            first_row = (block * TOK_DEV).astype(jnp.int32)
            q_block = lax.dynamic_slice_in_dim(query_rot, first_row, TOK_DEV, 0)
            q_doc = lax.dynamic_slice_in_dim(query_doc, first_row, TOK_DEV, 0)
            q_index = lax.dynamic_slice_in_dim(token_index, first_row, TOK_DEV, 0)
            k_block = lax.dynamic_slice_in_dim(key_rot, first_row, margin + TOK_DEV, 0)
            v_block = lax.dynamic_slice_in_dim(value_padded, first_row, margin + TOK_DEV, 0)
            k_doc = lax.dynamic_slice_in_dim(key_doc, first_row, margin + TOK_DEV, 0)
            k_index = lax.dynamic_slice_in_dim(padded_index, first_row, margin + TOK_DEV, 0)
            return attend(q_block, k_block, v_block, q_doc, q_index, k_doc, k_index)
        blocks = lax.map(per_block, jnp.arange(N_DOC, dtype=jnp.int32))
        return blocks.reshape(TOKENS, H * HD)
    return lax.map(per_candidate, factors)
```

```python
import math

import jax
import jax.numpy as jnp
from jax import lax
from jax.sharding import PartitionSpec as P

H = 64
KVH = 8
HD = 128
SPAN = 8


ROPE_BASE = 500000.0


def passed_along(value, axis, steps):
    count = lax.axis_size(axis)
    first, last = (max(0, -steps), min(count, count - steps))
    return lax.ppermute(value, axis, [(source, source + steps) for source in range(first, last)])


def locate(index_rows, lengths):
    ends = jnp.cumsum(lengths)
    starts = ends - lengths
    docid = jnp.sum((index_rows[:, None] >= ends[None, :]).astype(jnp.int32), axis=1)
    onehot = docid[:, None] == jnp.arange(lengths.shape[0], dtype=jnp.int32)[None, :]
    first_row = jnp.sum(jnp.where(onehot, starts[None, :], 0), axis=1)
    valid = index_rows >= 0
    return (jnp.where(valid, docid, -1), jnp.where(valid, index_rows - first_row, 0))


def rotate(values, offsets, factor):
    row_count = values.shape[0]
    heads_here = values.shape[1] // HD
    half_dim = HD // 2
    shaped = values.reshape(row_count, heads_here, HD).astype(jnp.float32)
    inverse = jnp.power(ROPE_BASE, -2.0 * jnp.arange(half_dim, dtype=jnp.float32) / HD) / factor
    angles = offsets.astype(jnp.float32)[:, None] * inverse[None, :]
    cosine = jnp.cos(angles)[:, None, :]
    sine = jnp.sin(angles)[:, None, :]
    first_half = shaped[..., :half_dim]
    second_half = shaped[..., half_dim:]
    turned = jnp.concatenate(
        [first_half * cosine - second_half * sine, second_half * cosine + first_half * sine],
        axis=-1,
    )
    return turned.reshape(row_count, heads_here * HD).astype(jnp.bfloat16)


def attend_group(query_rot, key_rot, value_rows, allowed):
    row_count = query_rot.shape[0]
    group_size = H // KVH
    q_part = query_rot.reshape(row_count, group_size, HD)
    scale = 1.0 / math.sqrt(HD)
    scores = jnp.einsum("rgd,wd->rgw", q_part, key_rot, preferred_element_type=jnp.float32) * scale
    scores = jnp.where(allowed[:, None, :], scores, -1e30)
    largest = jnp.max(scores, axis=-1, keepdims=True)
    expw = jnp.exp(scores - largest)
    total = jnp.sum(expw, axis=-1, keepdims=True)
    weights = expw.astype(jnp.bfloat16)
    numer = jnp.einsum("rgw,wd->rgd", weights, value_rows, preferred_element_type=jnp.float32)
    return (numer / total).astype(jnp.bfloat16).reshape(row_count, group_size * HD)


def on_device(queries, keys_values, factors, lengths):
    row_count = queries.shape[0]
    group_width = queries.shape[1] // KVH
    device = lax.axis_index("doc")
    group = lax.axis_index("cand")
    query_index = device * row_count + jnp.arange(row_count, dtype=jnp.int32)
    key_index = (device - SPAN) * row_count + jnp.arange((SPAN + 1) * row_count, dtype=jnp.int32)
    every_factor = lax.all_gather(factors, "cand", axis=0, tiled=True)
    pieces = []
    for distance in range(SPAN, 0, -1):
        pieces.append(passed_along(keys_values, "doc", distance))
    pieces.append(keys_values)
    window = jnp.concatenate(pieces, axis=1)
    query_doc, query_offset = locate(query_index, lengths)
    key_doc, key_offset = locate(key_index, lengths)
    allowed = (
        (key_doc[None, :] == query_doc[:, None])
        & (key_index[None, :] <= query_index[:, None])
        & (key_doc[None, :] >= 0)
    )
    own_queries = lax.dynamic_slice_in_dim(queries, group * group_width, group_width, 1)

    def per_candidate(factor):
        query_rot = rotate(own_queries, query_offset, factor)
        key_rot = rotate(window[0], key_offset, factor)
        return attend_group(query_rot, key_rot, window[1], allowed)

    mixed = lax.map(per_candidate, every_factor)
    return lax.all_to_all(mixed, "cand", 0, 2, tiled=True)


def solution(mesh):
    placed = (P("doc", None), P(None, "doc", "cand"), P("cand", None), P())
    return jax.shard_map(
        on_device, mesh=mesh, in_specs=placed, out_specs=P("cand", "doc", None), check_vma=False
    )
```

```python
import math

import jax
import jax.numpy as jnp
from jax import lax
from jax.experimental import pallas as pl
from jax.experimental.pallas import tpu as pltpu
from jax.sharding import PartitionSpec as P

H = 64
KVH = 8
HD = 128
SPAN = 8


ROPE_BASE = 500000.0


def passed_along(value, axis, steps):
    count = lax.axis_size(axis)
    first, last = (max(0, -steps), min(count, count - steps))
    return lax.ppermute(value, axis, [(source, source + steps) for source in range(first, last)])


def locate(index_rows, lengths):
    ends = jnp.cumsum(lengths)
    starts = ends - lengths
    docid = jnp.sum((index_rows[:, None] >= ends[None, :]).astype(jnp.int32), axis=1)
    onehot = docid[:, None] == jnp.arange(lengths.shape[0], dtype=jnp.int32)[None, :]
    first_row = jnp.sum(jnp.where(onehot, starts[None, :], 0), axis=1)
    valid = index_rows >= 0
    return (jnp.where(valid, docid, -1), jnp.where(valid, index_rows - first_row, 0))


def rotation_table(offsets, factors):
    half_dim = HD // 2
    inverse = jnp.power(ROPE_BASE, -2.0 * jnp.arange(half_dim, dtype=jnp.float32) / HD) / factors
    angles = offsets.astype(jnp.float32)[None, :, None] * inverse[:, None, :]
    return jnp.concatenate([jnp.cos(angles), jnp.sin(angles)], axis=-1)


def attention_kernel(q_ref, kv_ref, table_ref, bias_ref, out_ref):
    half_dim = HD // 2
    group_size = H // KVH
    query_rows = q_ref.shape[0]
    table = table_ref[0]
    swapped = pltpu.roll(table, half_dim, 1)
    low = lax.broadcasted_iota(jnp.int32, table.shape, 1) < half_dim
    cosine = jnp.where(low, table, swapped)
    sine = jnp.where(low, -swapped, table)
    keys = kv_ref[0].astype(jnp.float32)
    key_rot = (keys * cosine + pltpu.roll(keys, half_dim, 1) * sine).astype(jnp.bfloat16)
    values = kv_ref[1]
    first_query = table.shape[0] - query_rows
    q_cos = cosine[first_query:]
    q_sin = sine[first_query:]
    bias = bias_ref[...]
    scale = 1.0 / math.sqrt(HD)
    for head in range(group_size):
        cols = slice(head * HD, (head + 1) * HD)
        x = q_ref[:, cols].astype(jnp.float32)
        q_rot = (x * q_cos + pltpu.roll(x, half_dim, 1) * q_sin).astype(jnp.bfloat16)
        scores = lax.dot_general(
            q_rot, key_rot, (((1,), (1,)), ((), ())), preferred_element_type=jnp.float32
        )
        scores = scores * scale + bias
        largest = jnp.max(scores, axis=-1, keepdims=True)
        expw = jnp.exp(scores - largest)
        total = jnp.sum(expw, axis=-1, keepdims=True)
        numer = jnp.dot(expw.astype(jnp.bfloat16), values, preferred_element_type=jnp.float32)
        out_ref[0, :, cols] = (numer / total).astype(jnp.bfloat16)


def attend_all(own_queries, window, table, bias):
    cands, key_rows, _ = table.shape
    query_rows, width = own_queries.shape
    heads = width // HD
    flops = cands * heads * 4 * query_rows * key_rows * HD
    return pl.pallas_call(
        attention_kernel,
        out_shape=jax.ShapeDtypeStruct((cands, query_rows, width), jnp.bfloat16),
        grid=(cands,),
        in_specs=[
            pl.BlockSpec((query_rows, width), lambda c: (0, 0)),
            pl.BlockSpec(window.shape, lambda c: (0, 0, 0)),
            pl.BlockSpec((1, key_rows, HD), lambda c: (c, 0, 0)),
            pl.BlockSpec(bias.shape, lambda c: (0, 0)),
        ],
        out_specs=pl.BlockSpec((1, query_rows, width), lambda c: (c, 0, 0)),
        cost_estimate=pl.CostEstimate(
            flops=flops,
            transcendentals=cands * heads * query_rows * key_rows,
            bytes_accessed=table.size * 4 + window.size * 2 + cands * query_rows * width * 2,
        ),
    )(own_queries, window, table, bias)


def on_device(queries, keys_values, factors, lengths):
    row_count = queries.shape[0]
    group_width = queries.shape[1] // KVH
    device = lax.axis_index("doc")
    group = lax.axis_index("cand")
    query_index = device * row_count + jnp.arange(row_count, dtype=jnp.int32)
    key_index = (device - SPAN) * row_count + jnp.arange((SPAN + 1) * row_count, dtype=jnp.int32)
    every_factor = lax.all_gather(factors, "cand", axis=0, tiled=True)
    pieces = []
    for distance in range(SPAN, 0, -1):
        pieces.append(passed_along(keys_values, "doc", distance))
    pieces.append(keys_values)
    window = jnp.concatenate(pieces, axis=1)
    query_doc, _ = locate(query_index, lengths)
    key_doc, key_offset = locate(key_index, lengths)
    allowed = (
        (key_doc[None, :] == query_doc[:, None])
        & (key_index[None, :] <= query_index[:, None])
        & (key_doc[None, :] >= 0)
    )
    bias = jnp.where(allowed, 0.0, -1e30).astype(jnp.float32)
    table = rotation_table(key_offset, every_factor)
    own_queries = lax.dynamic_slice_in_dim(queries, group * group_width, group_width, 1)
    mixed = attend_all(own_queries, window, table, bias)
    return lax.all_to_all(mixed, "cand", 0, 2, tiled=True)


def solution(mesh):
    placed = (P("doc", None), P(None, "doc", "cand"), P("cand", None), P())
    return jax.shard_map(
        on_device, mesh=mesh, in_specs=placed, out_specs=P("cand", "doc", None), check_vma=False
    )
```

```python
import math

import jax
import jax.numpy as jnp
from jax import lax
from jax.experimental import pallas as pl
from jax.experimental.pallas import tpu as pltpu
from jax.sharding import PartitionSpec as P

H = 64
KVH = 8
HD = 128
SPAN = 8


ROPE_BASE = 500000.0


def passed_along(value, axis, steps):
    count = lax.axis_size(axis)
    first, last = (max(0, -steps), min(count, count - steps))
    return lax.ppermute(value, axis, [(source, source + steps) for source in range(first, last)])


def locate(index_rows, lengths):
    ends = jnp.cumsum(lengths)
    starts = ends - lengths
    docid = jnp.sum((index_rows[:, None] >= ends[None, :]).astype(jnp.int32), axis=1)
    onehot = docid[:, None] == jnp.arange(lengths.shape[0], dtype=jnp.int32)[None, :]
    first_row = jnp.sum(jnp.where(onehot, starts[None, :], 0), axis=1)
    valid = index_rows >= 0
    return (jnp.where(valid, docid, -1), jnp.where(valid, index_rows - first_row, 0))


def inverse_rows(factors):
    half_dim = HD // 2
    inverse = jnp.power(ROPE_BASE, -2.0 * jnp.arange(half_dim, dtype=jnp.float32) / HD) / factors
    return jnp.concatenate([inverse, inverse], axis=-1)[:, None, :]


def cos_and_sin(angle, low):
    turns = jnp.floor(angle * 0.636619772367581343 + 0.5)
    rest = ((angle - turns * 1.5703125) - turns * 4.837512969970703125e-4) - turns * 7.54978995489188216e-8
    square = rest * rest
    sine = rest + rest * square * (-1.6666654611e-1 + square * (8.3321608736e-3 + square * -1.9515295891e-4))
    cosine = 1.0 - 0.5 * square + square * square * (
        4.166664568298827e-2 + square * (-1.388731625493765e-3 + square * 2.443315711809948e-5)
    )
    quadrant = turns.astype(jnp.int32) + jnp.where(low, 0, 3)
    base = jnp.where((quadrant & 1) == 1, sine, cosine)
    return jnp.where(((quadrant + 1) & 2) != 0, -base, base)


def attention_kernel(q_ref, kv_ref, offset_ref, inverse_ref, bias_ref, out_ref):
    half_dim = HD // 2
    group_size = H // KVH
    query_rows = q_ref.shape[0]
    angle = offset_ref[...] * inverse_ref[0]
    low = lax.broadcasted_iota(jnp.int32, angle.shape, 1) < half_dim
    table = cos_and_sin(angle, low)
    swapped = pltpu.roll(table, half_dim, 1)
    cosine = jnp.where(low, table, swapped)
    sine = jnp.where(low, -swapped, table)
    keys = kv_ref[0].astype(jnp.float32)
    key_rot = (keys * cosine + pltpu.roll(keys, half_dim, 1) * sine).astype(jnp.bfloat16)
    values = kv_ref[1]
    first_query = angle.shape[0] - query_rows
    q_cos = cosine[first_query:]
    q_sin = sine[first_query:]
    bias = bias_ref[...]
    scale = 1.0 / math.sqrt(HD)
    for head in range(group_size):
        cols = slice(head * HD, (head + 1) * HD)
        x = q_ref[:, cols].astype(jnp.float32)
        q_rot = (x * q_cos + pltpu.roll(x, half_dim, 1) * q_sin).astype(jnp.bfloat16)
        scores = lax.dot_general(
            q_rot, key_rot, (((1,), (1,)), ((), ())), preferred_element_type=jnp.float32
        )
        scores = scores * scale + bias
        largest = jnp.max(scores, axis=-1, keepdims=True)
        expw = jnp.exp(scores - largest)
        total = jnp.sum(expw, axis=-1, keepdims=True)
        numer = jnp.dot(expw.astype(jnp.bfloat16), values, preferred_element_type=jnp.float32)
        out_ref[0, :, cols] = (numer / total).astype(jnp.bfloat16)


def attend_all(own_queries, window, offsets, inverse, bias):
    cands = inverse.shape[0]
    key_rows = window.shape[1]
    query_rows, width = own_queries.shape
    heads = width // HD
    flops = cands * heads * 4 * query_rows * key_rows * HD
    return pl.pallas_call(
        attention_kernel,
        out_shape=jax.ShapeDtypeStruct((cands, query_rows, width), jnp.bfloat16),
        grid=(cands,),
        in_specs=[
            pl.BlockSpec((query_rows, width), lambda c: (0, 0)),
            pl.BlockSpec(window.shape, lambda c: (0, 0, 0)),
            pl.BlockSpec(offsets.shape, lambda c: (0, 0)),
            pl.BlockSpec((1, 1, HD), lambda c: (c, 0, 0)),
            pl.BlockSpec(bias.shape, lambda c: (0, 0)),
        ],
        out_specs=pl.BlockSpec((1, query_rows, width), lambda c: (c, 0, 0)),
        cost_estimate=pl.CostEstimate(
            flops=flops,
            transcendentals=cands * heads * query_rows * key_rows,
            bytes_accessed=window.size * 2 + own_queries.size * 2 + cands * query_rows * width * 2,
        ),
    )(own_queries, window, offsets, inverse, bias)


def cyclic_shift(value, axis, steps):
    count = lax.axis_size(axis)
    return lax.ppermute(value, axis, [(source, (source + steps) % count) for source in range(count)])


def on_device(queries, keys_values, factors, lengths):
    row_count = queries.shape[0]
    group_width = queries.shape[1] // KVH
    device = lax.axis_index("doc")
    group = lax.axis_index("cand")
    query_index = device * row_count + jnp.arange(row_count, dtype=jnp.int32)
    key_index = (device - SPAN) * row_count + jnp.arange((SPAN + 1) * row_count, dtype=jnp.int32)
    cands = lax.axis_size("cand")
    behind = factors
    reach = 1
    while reach < cands:
        behind = jnp.concatenate([behind, cyclic_shift(behind, "cand", reach)], axis=0)
        reach *= 2
    every_factor = jnp.take(behind, (group - jnp.arange(cands, dtype=jnp.int32)) % cands, axis=0)
    far = passed_along(keys_values, "doc", SPAN)
    window = keys_values
    reach = 1
    while reach < SPAN:
        window = jnp.concatenate([passed_along(window, "doc", reach), window], axis=1)
        reach *= 2
    window = jnp.concatenate([far, window], axis=1)
    query_doc, _ = locate(query_index, lengths)
    key_doc, key_offset = locate(key_index, lengths)
    allowed = (
        (key_doc[None, :] == query_doc[:, None])
        & (key_index[None, :] <= query_index[:, None])
        & (key_doc[None, :] >= 0)
    )
    bias = jnp.where(allowed, 0.0, -1e30).astype(jnp.float32)
    offsets = jnp.broadcast_to(key_offset.astype(jnp.float32)[:, None], (key_offset.shape[0], HD))
    own_queries = lax.dynamic_slice_in_dim(queries, group * group_width, group_width, 1)
    mixed = attend_all(own_queries, window, offsets, inverse_rows(every_factor), bias)
    return lax.all_to_all(mixed, "cand", 0, 2, tiled=True)


def solution(mesh):
    placed = (P("doc", None), P(None, "doc", "cand"), P("cand", None), P())
    return jax.shard_map(
        on_device, mesh=mesh, in_specs=placed, out_specs=P("cand", "doc", None), check_vma=False
    )
```

```python
import math

import jax
import jax.numpy as jnp
from jax import lax
from jax.experimental import pallas as pl
from jax.experimental.pallas import tpu as pltpu
from jax.sharding import PartitionSpec as P

H = 64
KVH = 8
HD = 128
SPAN = 8


ROPE_BASE = 500000.0


def passed_along(value, axis, steps):
    count = lax.axis_size(axis)
    first, last = (max(0, -steps), min(count, count - steps))
    return lax.ppermute(value, axis, [(source, source + steps) for source in range(first, last)])


def locate(index_rows, lengths):
    ends = jnp.cumsum(lengths)
    starts = ends - lengths
    docid = jnp.sum((index_rows[:, None] >= ends[None, :]).astype(jnp.int32), axis=1)
    onehot = docid[:, None] == jnp.arange(lengths.shape[0], dtype=jnp.int32)[None, :]
    first_row = jnp.sum(jnp.where(onehot, starts[None, :], 0), axis=1)
    valid = index_rows >= 0
    return (jnp.where(valid, docid, -1), jnp.where(valid, index_rows - first_row, 0))


def inverse_rows(factors):
    half_dim = HD // 2
    inverse = jnp.power(ROPE_BASE, -2.0 * jnp.arange(half_dim, dtype=jnp.float32) / HD) / factors
    return jnp.concatenate([inverse, inverse], axis=-1)[:, None, :]


def cos_and_sin(angle, low):
    turns = jnp.floor(angle * 0.636619772367581343 + 0.5)
    rest = ((angle - turns * 1.5703125) - turns * 4.837512969970703125e-4) - turns * 7.54978995489188216e-8
    square = rest * rest
    sine = rest + rest * square * (-1.6666654611e-1 + square * (8.3321608736e-3 + square * -1.9515295891e-4))
    cosine = 1.0 - 0.5 * square + square * square * (
        4.166664568298827e-2 + square * (-1.388731625493765e-3 + square * 2.443315711809948e-5)
    )
    quadrant = turns.astype(jnp.int32) + jnp.where(low, 0, 3)
    base = jnp.where((quadrant & 1) == 1, sine, cosine)
    return jnp.where(((quadrant + 1) & 2) != 0, -base, base)


def attention_kernel(q_ref, kv_ref, offset_ref, inverse_ref, bias_ref, out_ref):
    half_dim = HD // 2
    group_size = H // KVH
    query_rows = q_ref.shape[0]
    angle = offset_ref[...] * inverse_ref[0]
    low = lax.broadcasted_iota(jnp.int32, angle.shape, 1) < half_dim
    table = cos_and_sin(angle, low)
    swapped = pltpu.roll(table, half_dim, 1)
    cosine = jnp.where(low, table, swapped)
    sine = jnp.where(low, -swapped, table)
    keys = kv_ref[0].astype(jnp.float32)
    key_rot = (keys * cosine + pltpu.roll(keys, half_dim, 1) * sine).astype(jnp.bfloat16)
    values = kv_ref[1]
    first_query = angle.shape[0] - query_rows
    q_cos = cosine[first_query:]
    q_sin = sine[first_query:]
    bias = bias_ref[...]
    scale = 1.0 / math.sqrt(HD)
    for head in range(group_size):
        cols = slice(head * HD, (head + 1) * HD)
        x = q_ref[:, cols].astype(jnp.float32)
        q_rot = (x * q_cos + pltpu.roll(x, half_dim, 1) * q_sin).astype(jnp.bfloat16)
        scores = lax.dot_general(
            q_rot, key_rot, (((1,), (1,)), ((), ())), preferred_element_type=jnp.float32
        )
        scores = scores * scale + bias
        largest = jnp.max(scores, axis=-1, keepdims=True)
        expw = jnp.exp(scores - largest)
        total = jnp.sum(expw, axis=-1, keepdims=True)
        numer = jnp.dot(expw.astype(jnp.bfloat16), values, preferred_element_type=jnp.float32)
        out_ref[0, :, cols] = (numer / total).astype(jnp.bfloat16)


def attend_all(own_queries, window, offsets, inverse, bias):
    cands = inverse.shape[0]
    key_rows = window.shape[1]
    query_rows, width = own_queries.shape
    heads = width // HD
    flops = cands * heads * 4 * query_rows * key_rows * HD
    return pl.pallas_call(
        attention_kernel,
        out_shape=jax.ShapeDtypeStruct((cands, query_rows, width), jnp.bfloat16),
        grid=(cands,),
        in_specs=[
            pl.BlockSpec((query_rows, width), lambda c: (0, 0)),
            pl.BlockSpec(window.shape, lambda c: (0, 0, 0)),
            pl.BlockSpec(offsets.shape, lambda c: (0, 0)),
            pl.BlockSpec((1, 1, HD), lambda c: (c, 0, 0)),
            pl.BlockSpec(bias.shape, lambda c: (0, 0)),
        ],
        out_specs=pl.BlockSpec((1, query_rows, width), lambda c: (c, 0, 0)),
        cost_estimate=pl.CostEstimate(
            flops=flops,
            transcendentals=cands * heads * query_rows * key_rows,
            bytes_accessed=window.size * 2 + own_queries.size * 2 + cands * query_rows * width * 2,
        ),
    )(own_queries, window, offsets, inverse, bias)


def cyclic_shift(value, axis, steps):
    count = lax.axis_size(axis)
    return lax.ppermute(value, axis, [(source, (source + steps) % count) for source in range(count)])


def on_device(queries, keys_values, factors, lengths):
    row_count = queries.shape[0]
    group_width = queries.shape[1] // KVH
    device = lax.axis_index("doc")
    group = lax.axis_index("cand")
    query_index = device * row_count + jnp.arange(row_count, dtype=jnp.int32)
    key_index = (device - SPAN) * row_count + jnp.arange((SPAN + 1) * row_count, dtype=jnp.int32)
    cands = lax.axis_size("cand")
    behind = factors
    reach = 1
    while reach < cands:
        behind = jnp.concatenate([behind, cyclic_shift(behind, "cand", reach)], axis=0)
        reach *= 2
    far = passed_along(keys_values, "doc", SPAN)
    window = keys_values
    reach = 1
    while reach < SPAN:
        window = jnp.concatenate([passed_along(window, "doc", reach), window], axis=1)
        reach *= 2
    window = jnp.concatenate([far, window], axis=1)
    query_doc, _ = locate(query_index, lengths)
    key_doc, key_offset = locate(key_index, lengths)
    allowed = (
        (key_doc[None, :] == query_doc[:, None])
        & (key_index[None, :] <= query_index[:, None])
        & (key_doc[None, :] >= 0)
    )
    bias = jnp.where(allowed, 0.0, -1e30).astype(jnp.float32)
    offsets = jnp.broadcast_to(key_offset.astype(jnp.float32)[:, None], (key_offset.shape[0], HD))
    own_queries = lax.dynamic_slice_in_dim(queries, group * group_width, group_width, 1)
    placed = jnp.zeros((row_count, queries.shape[1]), jnp.bfloat16)
    order = list(range(1, cands)) + [0]
    chunk = 2
    for first in range(0, cands, chunk):
        steps = order[first : first + chunk]
        rows = jnp.concatenate([inverse_for(behind, step) for step in steps], axis=0)
        mixed = attend_all(own_queries, window, offsets, rows, bias)
        for slot, step in enumerate(steps):
            block = mixed[slot]
            if step:
                block = cyclic_shift(block, "cand", step)
            source = (group - step) % cands
            placed = lax.dynamic_update_slice_in_dim(placed, block, source * group_width, 1)
    return placed[None]


def inverse_for(behind, step):
    count = behind.shape[0]
    return inverse_rows(behind[(count - step) % count :][:1])


def solution(mesh):
    placed = (P("doc", None), P(None, "doc", "cand"), P("cand", None), P())
    return jax.shard_map(
        on_device, mesh=mesh, in_specs=placed, out_specs=P("cand", "doc", None), check_vma=False
    )
```

```python
import math

import jax
import jax.numpy as jnp
from jax import lax
from jax.experimental import pallas as pl
from jax.experimental.pallas import tpu as pltpu
from jax.sharding import PartitionSpec as P

H = 64
KVH = 8
HD = 128
SPAN = 8


ROPE_BASE = 500000.0


def passed_along(value, axis, steps):
    count = lax.axis_size(axis)
    first, last = (max(0, -steps), min(count, count - steps))
    return lax.ppermute(value, axis, [(source, source + steps) for source in range(first, last)])


def locate(index_rows, lengths):
    ends = jnp.cumsum(lengths)
    starts = ends - lengths
    docid = jnp.sum((index_rows[:, None] >= ends[None, :]).astype(jnp.int32), axis=1)
    onehot = docid[:, None] == jnp.arange(lengths.shape[0], dtype=jnp.int32)[None, :]
    first_row = jnp.sum(jnp.where(onehot, starts[None, :], 0), axis=1)
    valid = index_rows >= 0
    return (jnp.where(valid, docid, -1), jnp.where(valid, index_rows - first_row, 0))


def inverse_rows(factors):
    half_dim = HD // 2
    inverse = jnp.power(ROPE_BASE, -2.0 * jnp.arange(half_dim, dtype=jnp.float32) / HD) / factors
    return jnp.concatenate([inverse, inverse], axis=-1)[:, None, :]


def cos_and_sin(angle, low):
    turns = jnp.floor(angle * 0.636619772367581343 + 0.5)
    rest = ((angle - turns * 1.5703125) - turns * 4.837512969970703125e-4) - turns * 7.54978995489188216e-8
    square = rest * rest
    sine = rest + rest * square * (-1.6666654611e-1 + square * (8.3321608736e-3 + square * -1.9515295891e-4))
    cosine = 1.0 - 0.5 * square + square * square * (
        4.166664568298827e-2 + square * (-1.388731625493765e-3 + square * 2.443315711809948e-5)
    )
    quadrant = turns.astype(jnp.int32) + jnp.where(low, 0, 3)
    base = jnp.where((quadrant & 1) == 1, sine, cosine)
    return jnp.where(((quadrant + 1) & 2) != 0, -base, base)


def attention_kernel(q_ref, kv_ref, offset_ref, inverse_ref, bias_ref, out_ref):
    half_dim = HD // 2
    group_size = H // KVH
    query_rows = q_ref.shape[0]
    angle = offset_ref[...] * inverse_ref[0]
    low = lax.broadcasted_iota(jnp.int32, angle.shape, 1) < half_dim
    table = cos_and_sin(angle, low)
    swapped = pltpu.roll(table, half_dim, 1)
    cosine = jnp.where(low, table, swapped)
    sine = jnp.where(low, -swapped, table)
    keys = kv_ref[0].astype(jnp.float32)
    key_rot = (keys * cosine + pltpu.roll(keys, half_dim, 1) * sine).astype(jnp.bfloat16)
    values = kv_ref[1]
    first_query = angle.shape[0] - query_rows
    q_cos = cosine[first_query:]
    q_sin = sine[first_query:]
    bias = bias_ref[...]
    scale = 1.0 / math.sqrt(HD)
    for head in range(group_size):
        cols = slice(head * HD, (head + 1) * HD)
        x = q_ref[:, cols].astype(jnp.float32)
        q_rot = (x * q_cos + pltpu.roll(x, half_dim, 1) * q_sin).astype(jnp.bfloat16)
        scores = lax.dot_general(
            q_rot, key_rot, (((1,), (1,)), ((), ())), preferred_element_type=jnp.float32
        )
        scores = scores * scale + bias
        largest = jnp.max(scores, axis=-1, keepdims=True)
        expw = jnp.exp(scores - largest)
        total = jnp.sum(expw, axis=-1, keepdims=True)
        numer = jnp.dot(expw.astype(jnp.bfloat16), values, preferred_element_type=jnp.float32)
        out_ref[0, :, cols] = (numer / total).astype(jnp.bfloat16)


def attend_all(own_queries, window, offsets, inverse, bias):
    cands = inverse.shape[0]
    key_rows = window.shape[1]
    query_rows, width = own_queries.shape
    heads = width // HD
    flops = cands * heads * 4 * query_rows * key_rows * HD
    return pl.pallas_call(
        attention_kernel,
        out_shape=jax.ShapeDtypeStruct((cands, query_rows, width), jnp.bfloat16),
        grid=(cands,),
        in_specs=[
            pl.BlockSpec((query_rows, width), lambda c: (0, 0)),
            pl.BlockSpec(window.shape, lambda c: (0, 0, 0)),
            pl.BlockSpec(offsets.shape, lambda c: (0, 0)),
            pl.BlockSpec((1, 1, HD), lambda c: (c, 0, 0)),
            pl.BlockSpec(bias.shape, lambda c: (0, 0)),
        ],
        out_specs=pl.BlockSpec((1, query_rows, width), lambda c: (c, 0, 0)),
        cost_estimate=pl.CostEstimate(
            flops=flops,
            transcendentals=cands * heads * query_rows * key_rows,
            bytes_accessed=window.size * 2 + own_queries.size * 2 + cands * query_rows * width * 2,
        ),
    )(own_queries, window, offsets, inverse, bias)


def place_kernel(in_ref, out_ref):
    out_ref[...] = in_ref[0]


def side_by_side(blocks):
    count, rows, width = blocks.shape
    return pl.pallas_call(
        place_kernel,
        out_shape=jax.ShapeDtypeStruct((rows, count * width), blocks.dtype),
        grid=(count,),
        in_specs=[pl.BlockSpec((1, rows, width), lambda g: (g, 0, 0))],
        out_specs=pl.BlockSpec((rows, width), lambda g: (0, g)),
    )(blocks)


def cyclic_shift(value, axis, steps):
    count = lax.axis_size(axis)
    return lax.ppermute(value, axis, [(source, (source + steps) % count) for source in range(count)])


def on_device(queries, keys_values, factors, lengths):
    row_count = queries.shape[0]
    group_width = queries.shape[1] // KVH
    device = lax.axis_index("doc")
    group = lax.axis_index("cand")
    query_index = device * row_count + jnp.arange(row_count, dtype=jnp.int32)
    key_index = (device - SPAN) * row_count + jnp.arange((SPAN + 1) * row_count, dtype=jnp.int32)
    cands = lax.axis_size("cand")
    every_factor = lax.all_to_all(
        jnp.broadcast_to(factors, (cands, factors.shape[1])), "cand", 0, 0, tiled=True
    )
    far = passed_along(keys_values, "doc", SPAN)
    window = keys_values
    reach = 1
    while reach < SPAN:
        window = jnp.concatenate([passed_along(window, "doc", reach), window], axis=1)
        reach *= 2
    window = jnp.concatenate([far, window], axis=1)
    query_doc, _ = locate(query_index, lengths)
    key_doc, key_offset = locate(key_index, lengths)
    allowed = (
        (key_doc[None, :] == query_doc[:, None])
        & (key_index[None, :] <= query_index[:, None])
        & (key_doc[None, :] >= 0)
    )
    bias = jnp.where(allowed, 0.0, -1e30).astype(jnp.float32)
    offsets = jnp.broadcast_to(key_offset.astype(jnp.float32)[:, None], (key_offset.shape[0], HD))
    own_queries = lax.dynamic_slice_in_dim(queries, group * group_width, group_width, 1)
    mixed = attend_all(own_queries, window, offsets, inverse_rows(every_factor), bias)
    gathered = lax.all_to_all(mixed, "cand", 0, 0, tiled=True)
    return side_by_side(gathered)[None]


def solution(mesh):
    placed = (P("doc", None), P(None, "doc", "cand"), P("cand", None), P())
    return jax.shard_map(
        on_device, mesh=mesh, in_specs=placed, out_specs=P("cand", "doc", None), check_vma=False
    )
```

```python
import math

import jax
import jax.numpy as jnp
from jax import lax
from jax.experimental import pallas as pl
from jax.experimental.pallas import tpu as pltpu
from jax.sharding import PartitionSpec as P

H = 64
KVH = 8
HD = 128
SPAN = 8


ROPE_BASE = 500000.0


def passed_along(value, axis, steps):
    count = lax.axis_size(axis)
    first, last = (max(0, -steps), min(count, count - steps))
    return lax.ppermute(value, axis, [(source, source + steps) for source in range(first, last)])


def locate(index_rows, lengths):
    ends = jnp.cumsum(lengths)
    starts = ends - lengths
    docid = jnp.sum((index_rows[:, None] >= ends[None, :]).astype(jnp.int32), axis=1)
    onehot = docid[:, None] == jnp.arange(lengths.shape[0], dtype=jnp.int32)[None, :]
    first_row = jnp.sum(jnp.where(onehot, starts[None, :], 0), axis=1)
    valid = index_rows >= 0
    return (jnp.where(valid, docid, -1), jnp.where(valid, index_rows - first_row, 0))


def inverse_rows(factors):
    half_dim = HD // 2
    inverse = jnp.power(ROPE_BASE, -2.0 * jnp.arange(half_dim, dtype=jnp.float32) / HD) / factors
    return jnp.concatenate([inverse, inverse], axis=-1)[:, None, :]


def cos_and_sin(angle, low):
    turns = jnp.floor(angle * 0.636619772367581343 + 0.5)
    rest = ((angle - turns * 1.5703125) - turns * 4.837512969970703125e-4) - turns * 7.54978995489188216e-8
    square = rest * rest
    sine = rest + rest * square * (-1.6666654611e-1 + square * (8.3321608736e-3 + square * -1.9515295891e-4))
    cosine = 1.0 - 0.5 * square + square * square * (
        4.166664568298827e-2 + square * (-1.388731625493765e-3 + square * 2.443315711809948e-5)
    )
    quadrant = turns.astype(jnp.int32) + jnp.where(low, 0, 3)
    base = jnp.where((quadrant & 1) == 1, sine, cosine)
    return jnp.where(((quadrant + 1) & 2) != 0, -base, base)


def rotation(angle):
    half_dim = HD // 2
    low = lax.broadcasted_iota(jnp.int32, angle.shape, 1) < half_dim
    table = cos_and_sin(angle, low)
    swapped = pltpu.roll(table, half_dim, 1)
    return jnp.where(low, table, swapped), jnp.where(low, -swapped, table)


def turned(values, cosine, sine):
    return (values * cosine + pltpu.roll(values, HD // 2, 1) * sine).astype(jnp.bfloat16)


def attend_rows(q_ref, key_rot, values, q_cos, q_sin, bias, out_ref):
    group_size = H // KVH
    scale = 1.0 / math.sqrt(HD)
    for head in range(group_size):
        cols = slice(head * HD, (head + 1) * HD)
        q_rot = turned(q_ref[:, cols].astype(jnp.float32), q_cos, q_sin)
        scores = lax.dot_general(
            q_rot, key_rot, (((1,), (1,)), ((), ())), preferred_element_type=jnp.float32
        )
        scores = scores * scale + bias
        largest = jnp.max(scores, axis=-1, keepdims=True)
        expw = jnp.exp(scores - largest)
        total = jnp.sum(expw, axis=-1, keepdims=True)
        numer = jnp.dot(expw.astype(jnp.bfloat16), values, preferred_element_type=jnp.float32)
        out_ref[0, :, cols] = (numer / total).astype(jnp.bfloat16)


def first_kernel(q_ref, kv_ref, offset_ref, inverse_ref, bias_ref, out_ref, keys_out_ref):
    query_rows = q_ref.shape[0]
    cosine, sine = rotation(offset_ref[...] * inverse_ref[0])
    key_rot = turned(kv_ref[0].astype(jnp.float32), cosine, sine)
    keys_out_ref[0] = key_rot
    first_query = offset_ref.shape[0] - 2 * query_rows
    q_cos = cosine[first_query : first_query + query_rows]
    q_sin = sine[first_query : first_query + query_rows]
    attend_rows(q_ref, key_rot, kv_ref[1], q_cos, q_sin, bias_ref[...], out_ref)


def second_kernel(q_ref, kv_ref, offset_ref, inverse_ref, bias_ref, keys_ref, out_ref):
    query_rows = q_ref.shape[0]
    first_query = offset_ref.shape[0] - query_rows
    q_cos, q_sin = rotation(offset_ref[first_query:, :] * inverse_ref[0])
    attend_rows(q_ref, keys_ref[0], kv_ref[1], q_cos, q_sin, bias_ref[...], out_ref)


def attend_all(own_queries, window, offsets, inverse, bias):
    cands = inverse.shape[0]
    key_rows = window.shape[1]
    query_rows, width = own_queries.shape
    half = query_rows // 2
    flops = cands * (width // HD) * 4 * half * key_rows * HD
    common = [
        pl.BlockSpec(window.shape, lambda c: (0, 0, 0)),
        pl.BlockSpec(offsets.shape, lambda c: (0, 0)),
        pl.BlockSpec((1, 1, HD), lambda c: (c, 0, 0)),
    ]
    out_spec = pl.BlockSpec((1, half, width), lambda c: (c, 0, 0))
    keys_spec = pl.BlockSpec((1, key_rows, HD), lambda c: (c, 0, 0))
    cost = pl.CostEstimate(
        flops=flops,
        transcendentals=cands * (width // HD) * half * key_rows,
        bytes_accessed=window.size * 2 + own_queries.size + cands * half * width * 2,
    )
    first, rotated = pl.pallas_call(
        first_kernel,
        out_shape=(
            jax.ShapeDtypeStruct((cands, half, width), jnp.bfloat16),
            jax.ShapeDtypeStruct((cands, key_rows, HD), jnp.bfloat16),
        ),
        grid=(cands,),
        in_specs=[pl.BlockSpec((half, width), lambda c: (0, 0))]
        + common
        + [pl.BlockSpec((half, key_rows), lambda c: (0, 0))],
        out_specs=(out_spec, keys_spec),
        cost_estimate=cost,
    )(own_queries, window, offsets, inverse, bias)
    first = lax.all_to_all(first, "cand", 0, 0, tiled=True)
    second = pl.pallas_call(
        second_kernel,
        out_shape=jax.ShapeDtypeStruct((cands, half, width), jnp.bfloat16),
        grid=(cands,),
        in_specs=[pl.BlockSpec((half, width), lambda c: (1, 0))]
        + common
        + [pl.BlockSpec((half, key_rows), lambda c: (1, 0)), keys_spec],
        out_specs=out_spec,
        cost_estimate=cost,
    )(own_queries, window, offsets, inverse, bias, rotated)
    second = lax.all_to_all(second, "cand", 0, 0, tiled=True)
    return first, second


def place_kernel(in_ref, out_ref):
    out_ref[...] = in_ref[0, 0]


def side_by_side(first, second):
    count, rows, width = first.shape
    both = jnp.stack([first, second])
    return pl.pallas_call(
        place_kernel,
        out_shape=jax.ShapeDtypeStruct((2 * rows, count * width), first.dtype),
        grid=(2, count),
        in_specs=[pl.BlockSpec((1, 1, rows, width), lambda h, g: (h, g, 0, 0))],
        out_specs=pl.BlockSpec((rows, width), lambda h, g: (h, g)),
    )(both)


def cyclic_shift(value, axis, steps):
    count = lax.axis_size(axis)
    return lax.ppermute(value, axis, [(source, (source + steps) % count) for source in range(count)])


def on_device(queries, keys_values, factors, lengths):
    row_count = queries.shape[0]
    group_width = queries.shape[1] // KVH
    device = lax.axis_index("doc")
    group = lax.axis_index("cand")
    query_index = device * row_count + jnp.arange(row_count, dtype=jnp.int32)
    key_index = (device - SPAN) * row_count + jnp.arange((SPAN + 1) * row_count, dtype=jnp.int32)
    cands = lax.axis_size("cand")
    every_factor = lax.all_to_all(
        jnp.broadcast_to(factors, (cands, factors.shape[1])), "cand", 0, 0, tiled=True
    )
    far = passed_along(keys_values, "doc", SPAN)
    window = keys_values
    reach = 1
    while reach < SPAN:
        window = jnp.concatenate([passed_along(window, "doc", reach), window], axis=1)
        reach *= 2
    window = jnp.concatenate([far, window], axis=1)
    query_doc, _ = locate(query_index, lengths)
    key_doc, key_offset = locate(key_index, lengths)
    allowed = (
        (key_doc[None, :] == query_doc[:, None])
        & (key_index[None, :] <= query_index[:, None])
        & (key_doc[None, :] >= 0)
    )
    bias = jnp.where(allowed, 0.0, -1e30).astype(jnp.float32)
    offsets = jnp.broadcast_to(key_offset.astype(jnp.float32)[:, None], (key_offset.shape[0], HD))
    own_queries = lax.dynamic_slice_in_dim(queries, group * group_width, group_width, 1)
    first, second = attend_all(own_queries, window, offsets, inverse_rows(every_factor), bias)
    return side_by_side(first, second)[None]


def solution(mesh):
    placed = (P("doc", None), P(None, "doc", "cand"), P("cand", None), P())
    return jax.shard_map(
        on_device, mesh=mesh, in_specs=placed, out_specs=P("cand", "doc", None), check_vma=False
    )
```

```python
import math

import jax
import jax.numpy as jnp
from jax import lax
from jax.experimental import pallas as pl
from jax.experimental.pallas import tpu as pltpu
from jax.sharding import PartitionSpec as P

H = 64
KVH = 8
HD = 128
SPAN = 8


ROPE_BASE = 500000.0


def passed_along(value, axis, steps):
    count = lax.axis_size(axis)
    first, last = (max(0, -steps), min(count, count - steps))
    return lax.ppermute(value, axis, [(source, source + steps) for source in range(first, last)])


def locate(index_rows, lengths):
    ends = jnp.cumsum(lengths)
    starts = ends - lengths
    docid = jnp.sum((index_rows[:, None] >= ends[None, :]).astype(jnp.int32), axis=1)
    onehot = docid[:, None] == jnp.arange(lengths.shape[0], dtype=jnp.int32)[None, :]
    first_row = jnp.sum(jnp.where(onehot, starts[None, :], 0), axis=1)
    valid = index_rows >= 0
    return (jnp.where(valid, docid, -1), jnp.where(valid, index_rows - first_row, 0))


def inverse_rows(factors):
    half_dim = HD // 2
    inverse = jnp.power(ROPE_BASE, -2.0 * jnp.arange(half_dim, dtype=jnp.float32) / HD) / factors
    return jnp.concatenate([inverse, inverse], axis=-1)[:, None, :]


def cos_and_sin(angle, low):
    turns = jnp.floor(angle * 0.636619772367581343 + 0.5)
    rest = ((angle - turns * 1.5703125) - turns * 4.837512969970703125e-4) - turns * 7.54978995489188216e-8
    square = rest * rest
    sine = rest + rest * square * (-1.6666654611e-1 + square * (8.3321608736e-3 + square * -1.9515295891e-4))
    cosine = 1.0 - 0.5 * square + square * square * (
        4.166664568298827e-2 + square * (-1.388731625493765e-3 + square * 2.443315711809948e-5)
    )
    quadrant = turns.astype(jnp.int32) + jnp.where(low, 0, 3)
    base = jnp.where((quadrant & 1) == 1, sine, cosine)
    return jnp.where(((quadrant + 1) & 2) != 0, -base, base)


def attention_kernel(q_ref, kv_ref, offset_ref, inverse_ref, bias_ref, out_ref):
    half_dim = HD // 2
    group_size = H // KVH
    query_rows = q_ref.shape[0]
    angle = offset_ref[...] * inverse_ref[0]
    low = lax.broadcasted_iota(jnp.int32, angle.shape, 1) < half_dim
    table = cos_and_sin(angle, low)
    swapped = pltpu.roll(table, half_dim, 1)
    cosine = jnp.where(low, table, swapped)
    sine = jnp.where(low, -swapped, table)
    keys = kv_ref[0].astype(jnp.float32)
    key_rot = (keys * cosine + pltpu.roll(keys, half_dim, 1) * sine).astype(jnp.bfloat16)
    values = kv_ref[1]
    first_query = angle.shape[0] - query_rows
    q_cos = cosine[first_query:]
    q_sin = sine[first_query:]
    bias = bias_ref[...]
    scale = 1.0 / math.sqrt(HD)
    stacked = jnp.concatenate(
        [
            (
                q_ref[:, head * HD : (head + 1) * HD].astype(jnp.float32) * q_cos
                + pltpu.roll(q_ref[:, head * HD : (head + 1) * HD].astype(jnp.float32), half_dim, 1) * q_sin
            ).astype(jnp.bfloat16)
            for head in range(group_size)
        ],
        axis=0,
    )
    scores = lax.dot_general(
        stacked, key_rot, (((1,), (1,)), ((), ())), preferred_element_type=jnp.float32
    )
    weights = []
    totals = []
    for head in range(group_size):
        part = scores[head * query_rows : (head + 1) * query_rows] * scale + bias
        largest = jnp.max(part, axis=-1, keepdims=True)
        expw = jnp.exp(part - largest)
        totals.append(jnp.sum(expw, axis=-1, keepdims=True))
        weights.append(expw.astype(jnp.bfloat16))
    numer = jnp.dot(jnp.concatenate(weights, axis=0), values, preferred_element_type=jnp.float32)
    for head in range(group_size):
        rows = numer[head * query_rows : (head + 1) * query_rows]
        out_ref[0, :, head * HD : (head + 1) * HD] = (rows / totals[head]).astype(jnp.bfloat16)


def attend_all(own_queries, window, offsets, inverse, bias):
    cands = inverse.shape[0]
    key_rows = window.shape[1]
    query_rows, width = own_queries.shape
    heads = width // HD
    flops = cands * heads * 4 * query_rows * key_rows * HD
    return pl.pallas_call(
        attention_kernel,
        out_shape=jax.ShapeDtypeStruct((cands, query_rows, width), jnp.bfloat16),
        grid=(cands,),
        in_specs=[
            pl.BlockSpec((query_rows, width), lambda c: (0, 0)),
            pl.BlockSpec(window.shape, lambda c: (0, 0, 0)),
            pl.BlockSpec(offsets.shape, lambda c: (0, 0)),
            pl.BlockSpec((1, 1, HD), lambda c: (c, 0, 0)),
            pl.BlockSpec(bias.shape, lambda c: (0, 0)),
        ],
        out_specs=pl.BlockSpec((1, query_rows, width), lambda c: (c, 0, 0)),
        cost_estimate=pl.CostEstimate(
            flops=flops,
            transcendentals=cands * heads * query_rows * key_rows,
            bytes_accessed=window.size * 2 + own_queries.size * 2 + cands * query_rows * width * 2,
        ),
    )(own_queries, window, offsets, inverse, bias)


def place_kernel(in_ref, out_ref):
    out_ref[...] = in_ref[0]


def side_by_side(blocks):
    count, rows, width = blocks.shape
    return pl.pallas_call(
        place_kernel,
        out_shape=jax.ShapeDtypeStruct((rows, count * width), blocks.dtype),
        grid=(count,),
        in_specs=[pl.BlockSpec((1, rows, width), lambda g: (g, 0, 0))],
        out_specs=pl.BlockSpec((rows, width), lambda g: (0, g)),
    )(blocks)


def cyclic_shift(value, axis, steps):
    count = lax.axis_size(axis)
    return lax.ppermute(value, axis, [(source, (source + steps) % count) for source in range(count)])


def on_device(queries, keys_values, factors, lengths):
    row_count = queries.shape[0]
    group_width = queries.shape[1] // KVH
    device = lax.axis_index("doc")
    group = lax.axis_index("cand")
    query_index = device * row_count + jnp.arange(row_count, dtype=jnp.int32)
    key_index = (device - SPAN) * row_count + jnp.arange((SPAN + 1) * row_count, dtype=jnp.int32)
    cands = lax.axis_size("cand")
    every_factor = lax.all_to_all(
        jnp.broadcast_to(factors, (cands, factors.shape[1])), "cand", 0, 0, tiled=True
    )
    far = passed_along(keys_values, "doc", SPAN)
    window = keys_values
    reach = 1
    while reach < SPAN:
        window = jnp.concatenate([passed_along(window, "doc", reach), window], axis=1)
        reach *= 2
    window = jnp.concatenate([far, window], axis=1)
    query_doc, _ = locate(query_index, lengths)
    key_doc, key_offset = locate(key_index, lengths)
    allowed = (
        (key_doc[None, :] == query_doc[:, None])
        & (key_index[None, :] <= query_index[:, None])
        & (key_doc[None, :] >= 0)
    )
    bias = jnp.where(allowed, 0.0, -1e30).astype(jnp.float32)
    offsets = jnp.broadcast_to(key_offset.astype(jnp.float32)[:, None], (key_offset.shape[0], HD))
    own_queries = lax.dynamic_slice_in_dim(queries, group * group_width, group_width, 1)
    mixed = attend_all(own_queries, window, offsets, inverse_rows(every_factor), bias)
    gathered = lax.all_to_all(mixed, "cand", 0, 0, tiled=True)
    return side_by_side(gathered)[None]


def solution(mesh):
    placed = (P("doc", None), P(None, "doc", "cand"), P("cand", None), P())
    return jax.shard_map(
        on_device, mesh=mesh, in_specs=placed, out_specs=P("cand", "doc", None), check_vma=False
    )
```

```python
import math

import jax
import jax.numpy as jnp
from jax import lax
from jax.experimental import pallas as pl
from jax.experimental.pallas import tpu as pltpu
from jax.sharding import PartitionSpec as P

H = 64
KVH = 8
HD = 128
SPAN = 8


ROPE_BASE = 500000.0


def passed_along(value, axis, steps):
    count = lax.axis_size(axis)
    first, last = (max(0, -steps), min(count, count - steps))
    return lax.ppermute(value, axis, [(source, source + steps) for source in range(first, last)])


def locate(index_rows, lengths):
    ends = jnp.cumsum(lengths)
    starts = ends - lengths
    docid = jnp.sum((index_rows[:, None] >= ends[None, :]).astype(jnp.int32), axis=1)
    onehot = docid[:, None] == jnp.arange(lengths.shape[0], dtype=jnp.int32)[None, :]
    first_row = jnp.sum(jnp.where(onehot, starts[None, :], 0), axis=1)
    valid = index_rows >= 0
    return (jnp.where(valid, docid, -1), jnp.where(valid, index_rows - first_row, 0))


def inverse_rows(factors):
    half_dim = HD // 2
    inverse = jnp.power(ROPE_BASE, -2.0 * jnp.arange(half_dim, dtype=jnp.float32) / HD) / factors
    return jnp.concatenate([inverse, inverse], axis=-1)[:, None, :]


def cos_and_sin(angle, low):
    turns = jnp.floor(angle * 0.636619772367581343 + 0.5)
    rest = ((angle - turns * 1.5703125) - turns * 4.837512969970703125e-4) - turns * 7.54978995489188216e-8
    square = rest * rest
    sine = rest + rest * square * (-1.6666654611e-1 + square * (8.3321608736e-3 + square * -1.9515295891e-4))
    cosine = 1.0 - 0.5 * square + square * square * (
        4.166664568298827e-2 + square * (-1.388731625493765e-3 + square * 2.443315711809948e-5)
    )
    quadrant = turns.astype(jnp.int32) + jnp.where(low, 0, 3)
    base = jnp.where((quadrant & 1) == 1, sine, cosine)
    return jnp.where(((quadrant + 1) & 2) != 0, -base, base)


def attention_kernel(q_ref, k_ref, vt_ref, offset_ref, inverse_ref, bias_ref, out_ref):
    half_dim = HD // 2
    group_size = H // KVH
    query_rows = q_ref.shape[0]
    angle = offset_ref[...] * inverse_ref[0]
    low = lax.broadcasted_iota(jnp.int32, angle.shape, 1) < half_dim
    table = cos_and_sin(angle, low)
    swapped = pltpu.roll(table, half_dim, 1)
    cosine = jnp.where(low, table, swapped)
    sine = jnp.where(low, -swapped, table)
    keys = k_ref[...].astype(jnp.float32)
    key_rot = (keys * cosine + pltpu.roll(keys, half_dim, 1) * sine).astype(jnp.bfloat16)
    first_query = angle.shape[0] - query_rows
    q_cos = cosine[first_query:]
    q_sin = sine[first_query:]
    bias = bias_ref[...]
    scale = 1.0 / math.sqrt(HD)
    stacked = jnp.concatenate(
        [
            (
                q_ref[:, head * HD : (head + 1) * HD].astype(jnp.float32) * q_cos
                + pltpu.roll(q_ref[:, head * HD : (head + 1) * HD].astype(jnp.float32), half_dim, 1) * q_sin
            ).astype(jnp.bfloat16)
            for head in range(group_size)
        ],
        axis=0,
    )
    scores = lax.dot_general(
        key_rot, stacked, (((1,), (1,)), ((), ())), preferred_element_type=jnp.float32
    )
    weights = []
    totals = []
    for head in range(group_size):
        part = scores[:, head * query_rows : (head + 1) * query_rows] * scale + bias
        largest = jnp.max(part, axis=0, keepdims=True)
        expw = jnp.exp(part - largest)
        totals.append(jnp.sum(expw, axis=0, keepdims=True))
        weights.append(expw.astype(jnp.bfloat16))
    numer = jnp.dot(vt_ref[...], jnp.concatenate(weights, axis=1), preferred_element_type=jnp.float32)
    for head in range(group_size):
        cols = numer[:, head * query_rows : (head + 1) * query_rows] / totals[head]
        out_ref[0, :, head * HD : (head + 1) * HD] = cols.T.astype(jnp.bfloat16)


def attend_all(own_queries, window, offsets, inverse, bias):
    keys = window[0]
    values_t = window[1].T
    cands = inverse.shape[0]
    key_rows = window.shape[1]
    query_rows, width = own_queries.shape
    heads = width // HD
    flops = cands * heads * 4 * query_rows * key_rows * HD
    return pl.pallas_call(
        attention_kernel,
        out_shape=jax.ShapeDtypeStruct((cands, query_rows, width), jnp.bfloat16),
        grid=(cands,),
        in_specs=[
            pl.BlockSpec((query_rows, width), lambda c: (0, 0)),
            pl.BlockSpec(keys.shape, lambda c: (0, 0)),
            pl.BlockSpec(values_t.shape, lambda c: (0, 0)),
            pl.BlockSpec(offsets.shape, lambda c: (0, 0)),
            pl.BlockSpec((1, 1, HD), lambda c: (c, 0, 0)),
            pl.BlockSpec(bias.T.shape, lambda c: (0, 0)),
        ],
        out_specs=pl.BlockSpec((1, query_rows, width), lambda c: (c, 0, 0)),
        cost_estimate=pl.CostEstimate(
            flops=flops,
            transcendentals=cands * heads * query_rows * key_rows,
            bytes_accessed=window.size * 2 + own_queries.size * 2 + cands * query_rows * width * 2,
        ),
    )(own_queries, keys, values_t, offsets, inverse, bias.T)


def place_kernel(in_ref, out_ref, flags):
    count, _, width = in_ref.shape
    copies = [
        pltpu.make_async_copy(in_ref.at[g], out_ref.at[:, pl.ds(g * width, width)], flags.at[g])
        for g in range(count)
    ]
    for copy in copies:
        copy.start()
    for copy in copies:
        copy.wait()


def side_by_side(blocks):
    count, rows, width = blocks.shape
    return pl.pallas_call(
        place_kernel,
        out_shape=jax.ShapeDtypeStruct((rows, count * width), blocks.dtype),
        in_specs=[pl.BlockSpec(memory_space=pl.ANY)],
        out_specs=pl.BlockSpec(memory_space=pl.ANY),
        scratch_shapes=[pltpu.SemaphoreType.DMA((count,))],
    )(blocks)


def cyclic_shift(value, axis, steps):
    count = lax.axis_size(axis)
    return lax.ppermute(value, axis, [(source, (source + steps) % count) for source in range(count)])


def on_device(queries, keys_values, factors, lengths):
    row_count = queries.shape[0]
    group_width = queries.shape[1] // KVH
    device = lax.axis_index("doc")
    group = lax.axis_index("cand")
    query_index = device * row_count + jnp.arange(row_count, dtype=jnp.int32)
    key_index = (device - SPAN) * row_count + jnp.arange((SPAN + 1) * row_count, dtype=jnp.int32)
    cands = lax.axis_size("cand")
    every_factor = lax.all_to_all(
        jnp.broadcast_to(factors, (cands, factors.shape[1])), "cand", 0, 0, tiled=True
    )
    far = passed_along(keys_values, "doc", SPAN)
    window = keys_values
    reach = 1
    while reach < SPAN:
        window = jnp.concatenate([passed_along(window, "doc", reach), window], axis=1)
        reach *= 2
    window = jnp.concatenate([far, window], axis=1)
    query_doc, _ = locate(query_index, lengths)
    key_doc, key_offset = locate(key_index, lengths)
    allowed = (
        (key_doc[None, :] == query_doc[:, None])
        & (key_index[None, :] <= query_index[:, None])
        & (key_doc[None, :] >= 0)
    )
    bias = jnp.where(allowed, 0.0, -1e30).astype(jnp.float32)
    offsets = jnp.broadcast_to(key_offset.astype(jnp.float32)[:, None], (key_offset.shape[0], HD))
    own_queries = lax.dynamic_slice_in_dim(queries, group * group_width, group_width, 1)
    mixed = attend_all(own_queries, window, offsets, inverse_rows(every_factor), bias)
    gathered = lax.all_to_all(mixed, "cand", 0, 0, tiled=True)
    return side_by_side(gathered)[None]


def solution(mesh):
    placed = (P("doc", None), P(None, "doc", "cand"), P("cand", None), P())
    return jax.shard_map(
        on_device, mesh=mesh, in_specs=placed, out_specs=P("cand", "doc", None), check_vma=False
    )
```

```python
import math

import jax
import jax.numpy as jnp
from jax import lax
from jax.experimental import pallas as pl
from jax.experimental.pallas import tpu as pltpu
from jax.sharding import PartitionSpec as P

H = 64
KVH = 8
HD = 128
SPAN = 8


ROPE_BASE = 500000.0


def passed_along(value, axis, steps):
    count = lax.axis_size(axis)
    first, last = (max(0, -steps), min(count, count - steps))
    return lax.ppermute(value, axis, [(source, source + steps) for source in range(first, last)])


def locate(index_rows, lengths):
    ends = jnp.cumsum(lengths)
    starts = ends - lengths
    docid = jnp.sum((index_rows[:, None] >= ends[None, :]).astype(jnp.int32), axis=1)
    onehot = docid[:, None] == jnp.arange(lengths.shape[0], dtype=jnp.int32)[None, :]
    first_row = jnp.sum(jnp.where(onehot, starts[None, :], 0), axis=1)
    valid = index_rows >= 0
    return (jnp.where(valid, docid, -1), jnp.where(valid, index_rows - first_row, 0))


def inverse_rows(factors):
    half_dim = HD // 2
    inverse = jnp.power(ROPE_BASE, -2.0 * jnp.arange(half_dim, dtype=jnp.float32) / HD) / factors
    return jnp.concatenate([inverse, inverse], axis=-1)[:, None, :]


def cos_and_sin(angle, low):
    turns = jnp.floor(angle * 0.636619772367581343 + 0.5)
    rest = ((angle - turns * 1.5703125) - turns * 4.837512969970703125e-4) - turns * 7.54978995489188216e-8
    square = rest * rest
    sine = rest + rest * square * (-1.6666654611e-1 + square * (8.3321608736e-3 + square * -1.9515295891e-4))
    cosine = 1.0 - 0.5 * square + square * square * (
        4.166664568298827e-2 + square * (-1.388731625493765e-3 + square * 2.443315711809948e-5)
    )
    quadrant = turns.astype(jnp.int32) + jnp.where(low, 0, 3)
    base = jnp.where((quadrant & 1) == 1, sine, cosine)
    return jnp.where(((quadrant + 1) & 2) != 0, -base, base)


def attention_kernel(q_ref, k_ref, vt_ref, offset_ref, inverse_ref, bias_ref, out_ref):
    half_dim = HD // 2
    group_size = H // KVH
    query_rows = q_ref.shape[0]
    angle = offset_ref[...] * inverse_ref[0]
    low = lax.broadcasted_iota(jnp.int32, angle.shape, 1) < half_dim
    table = cos_and_sin(angle, low)
    swapped = pltpu.roll(table, half_dim, 1)
    cosine = jnp.where(low, table, swapped)
    sine = jnp.where(low, -swapped, table)
    keys = k_ref[...].astype(jnp.float32)
    key_rot = (keys * cosine + pltpu.roll(keys, half_dim, 1) * sine).astype(jnp.bfloat16)
    first_query = angle.shape[0] - query_rows
    q_cos = cosine[first_query:]
    q_sin = sine[first_query:]
    bias = bias_ref[...]
    scale = 1.0 / math.sqrt(HD)
    stacked = jnp.concatenate(
        [
            (
                q_ref[:, head * HD : (head + 1) * HD].astype(jnp.float32) * q_cos
                + pltpu.roll(q_ref[:, head * HD : (head + 1) * HD].astype(jnp.float32), half_dim, 1) * q_sin
            ).astype(jnp.bfloat16)
            for head in range(group_size)
        ],
        axis=0,
    )
    scores = lax.dot_general(
        key_rot, stacked, (((1,), (1,)), ((), ())), preferred_element_type=jnp.float32
    )
    weights = []
    totals = []
    for head in range(group_size):
        part = scores[:, head * query_rows : (head + 1) * query_rows] * scale + bias
        largest = jnp.max(part, axis=0, keepdims=True)
        expw = jnp.exp(part - largest)
        totals.append(jnp.sum(expw, axis=0, keepdims=True))
        weights.append(expw.astype(jnp.bfloat16))
    numer = jnp.dot(vt_ref[...], jnp.concatenate(weights, axis=1), preferred_element_type=jnp.float32)
    for head in range(group_size):
        cols = numer[:, head * query_rows : (head + 1) * query_rows] / totals[head]
        out_ref[0, :, head * HD : (head + 1) * HD] = cols.T.astype(jnp.bfloat16)


def attend_all(own_queries, window, offsets, inverse, bias):
    keys = window[0]
    values_t = window[1].T
    cands = inverse.shape[0]
    key_rows = window.shape[1]
    query_rows, width = own_queries.shape
    heads = width // HD
    flops = cands * heads * 4 * query_rows * key_rows * HD
    return pl.pallas_call(
        attention_kernel,
        out_shape=jax.ShapeDtypeStruct((cands, query_rows, width), jnp.bfloat16),
        grid=(cands,),
        in_specs=[
            pl.BlockSpec((query_rows, width), lambda c: (0, 0)),
            pl.BlockSpec(keys.shape, lambda c: (0, 0)),
            pl.BlockSpec(values_t.shape, lambda c: (0, 0)),
            pl.BlockSpec(offsets.shape, lambda c: (0, 0)),
            pl.BlockSpec((1, 1, HD), lambda c: (c, 0, 0)),
            pl.BlockSpec(bias.T.shape, lambda c: (0, 0)),
        ],
        out_specs=pl.BlockSpec((1, query_rows, width), lambda c: (c, 0, 0)),
        cost_estimate=pl.CostEstimate(
            flops=flops,
            transcendentals=cands * heads * query_rows * key_rows,
            bytes_accessed=window.size * 2 + own_queries.size * 2 + cands * query_rows * width * 2,
        ),
    )(own_queries, keys, values_t, offsets, inverse, bias.T)


def place_kernel(in_ref, out_ref):
    out_ref[...] = in_ref[0]


def side_by_side(blocks):
    count, rows, width = blocks.shape
    return pl.pallas_call(
        place_kernel,
        out_shape=jax.ShapeDtypeStruct((rows, count * width), blocks.dtype),
        grid=(count,),
        in_specs=[pl.BlockSpec((1, rows, width), lambda g: (g, 0, 0))],
        out_specs=pl.BlockSpec((rows, width), lambda g: (0, g)),
    )(blocks)


def cyclic_shift(value, axis, steps):
    count = lax.axis_size(axis)
    return lax.ppermute(value, axis, [(source, (source + steps) % count) for source in range(count)])


def on_device(queries, keys_values, factors, lengths):
    row_count = queries.shape[0]
    group_width = queries.shape[1] // KVH
    device = lax.axis_index("doc")
    group = lax.axis_index("cand")
    query_index = device * row_count + jnp.arange(row_count, dtype=jnp.int32)
    key_index = (device - SPAN) * row_count + jnp.arange((SPAN + 1) * row_count, dtype=jnp.int32)
    cands = lax.axis_size("cand")
    every_factor = lax.all_to_all(
        jnp.broadcast_to(factors, (cands, factors.shape[1])), "cand", 0, 0, tiled=True
    )
    far = passed_along(keys_values, "doc", SPAN)
    window = keys_values
    reach = 1
    while reach < SPAN:
        window = jnp.concatenate([passed_along(window, "doc", reach), window], axis=1)
        reach *= 2
    window = jnp.concatenate([far, window], axis=1)
    query_doc, _ = locate(query_index, lengths)
    key_doc, key_offset = locate(key_index, lengths)
    allowed = (
        (key_doc[None, :] == query_doc[:, None])
        & (key_index[None, :] <= query_index[:, None])
        & (key_doc[None, :] >= 0)
    )
    bias = jnp.where(allowed, 0.0, -1e30).astype(jnp.float32)
    offsets = jnp.broadcast_to(key_offset.astype(jnp.float32)[:, None], (key_offset.shape[0], HD))
    own_queries = lax.dynamic_slice_in_dim(queries, group * group_width, group_width, 1)
    mixed = attend_all(own_queries, window, offsets, inverse_rows(every_factor), bias)
    gathered = lax.all_to_all(mixed, "cand", 0, 0, tiled=True)
    return side_by_side(gathered)[None]


def solution(mesh):
    placed = (P("doc", None), P(None, "doc", "cand"), P("cand", None), P())
    return jax.shard_map(
        on_device, mesh=mesh, in_specs=placed, out_specs=P("cand", "doc", None), check_vma=False
    )
```

```python
import math

import jax
import jax.numpy as jnp
from jax import lax
from jax.experimental import pallas as pl
from jax.experimental.pallas import tpu as pltpu
from jax.sharding import PartitionSpec as P

H = 64
KVH = 8
HD = 128
SPAN = 8


ROPE_BASE = 500000.0


def passed_along(value, axis, steps):
    count = lax.axis_size(axis)
    first, last = (max(0, -steps), min(count, count - steps))
    return lax.ppermute(value, axis, [(source, source + steps) for source in range(first, last)])


def locate(index_rows, lengths):
    ends = jnp.cumsum(lengths)
    starts = ends - lengths
    docid = jnp.sum((index_rows[:, None] >= ends[None, :]).astype(jnp.int32), axis=1)
    onehot = docid[:, None] == jnp.arange(lengths.shape[0], dtype=jnp.int32)[None, :]
    first_row = jnp.sum(jnp.where(onehot, starts[None, :], 0), axis=1)
    valid = index_rows >= 0
    return (jnp.where(valid, docid, -1), jnp.where(valid, index_rows - first_row, 0))


def inverse_rows(factors):
    half_dim = HD // 2
    inverse = jnp.power(ROPE_BASE, -2.0 * jnp.arange(half_dim, dtype=jnp.float32) / HD) / factors
    return jnp.concatenate([inverse, inverse], axis=-1)[:, None, :]


def cos_and_sin(angle, low):
    turns = jnp.floor(angle * 0.636619772367581343 + 0.5)
    rest = ((angle - turns * 1.5703125) - turns * 4.837512969970703125e-4) - turns * 7.54978995489188216e-8
    square = rest * rest
    sine = rest + rest * square * (-1.6666654611e-1 + square * (8.3321608736e-3 + square * -1.9515295891e-4))
    cosine = 1.0 - 0.5 * square + square * square * (
        4.166664568298827e-2 + square * (-1.388731625493765e-3 + square * 2.443315711809948e-5)
    )
    quadrant = turns.astype(jnp.int32) + jnp.where(low, 0, 3)
    base = jnp.where((quadrant & 1) == 1, sine, cosine)
    return jnp.where(((quadrant + 1) & 2) != 0, -base, base)


def attention_kernel(q_ref, k_ref, vt_ref, table_ref, bias_ref, out_ref):
    half_dim = HD // 2
    group_size = H // KVH
    query_rows = q_ref.shape[0]
    table = table_ref[0]
    low = lax.broadcasted_iota(jnp.int32, table.shape, 1) < half_dim
    swapped = pltpu.roll(table, half_dim, 1)
    cosine = jnp.where(low, table, swapped)
    sine = jnp.where(low, -swapped, table)
    keys = k_ref[...].astype(jnp.float32)
    key_rot = (keys * cosine + pltpu.roll(keys, half_dim, 1) * sine).astype(jnp.bfloat16)
    first_query = table.shape[0] - query_rows
    q_cos = cosine[first_query:]
    q_sin = sine[first_query:]
    bias = bias_ref[...]
    scale = 1.0 / math.sqrt(HD)
    stacked = jnp.concatenate(
        [
            (
                q_ref[:, head * HD : (head + 1) * HD].astype(jnp.float32) * q_cos
                + pltpu.roll(q_ref[:, head * HD : (head + 1) * HD].astype(jnp.float32), half_dim, 1) * q_sin
            ).astype(jnp.bfloat16)
            for head in range(group_size)
        ],
        axis=0,
    )
    scores = lax.dot_general(
        key_rot, stacked, (((1,), (1,)), ((), ())), preferred_element_type=jnp.float32
    )
    weights = []
    totals = []
    for head in range(group_size):
        part = scores[:, head * query_rows : (head + 1) * query_rows] * scale + bias
        largest = jnp.max(part, axis=0, keepdims=True)
        expw = jnp.exp(part - largest)
        totals.append(jnp.sum(expw, axis=0, keepdims=True))
        weights.append(expw.astype(jnp.bfloat16))
    numer = jnp.dot(vt_ref[...], jnp.concatenate(weights, axis=1), preferred_element_type=jnp.float32)
    for head in range(group_size):
        cols = numer[:, head * query_rows : (head + 1) * query_rows] / totals[head]
        out_ref[0, :, head * HD : (head + 1) * HD] = cols.T.astype(jnp.bfloat16)


def attend_all(own_queries, window, offsets, inverse, bias):
    angle = offsets[None] * inverse
    low = lax.broadcasted_iota(jnp.int32, angle.shape, 2) < HD // 2
    table = cos_and_sin(angle, low)
    keys = window[0]
    values_t = window[1].T
    cands = inverse.shape[0]
    key_rows = window.shape[1]
    query_rows, width = own_queries.shape
    heads = width // HD
    flops = cands * heads * 4 * query_rows * key_rows * HD
    return pl.pallas_call(
        attention_kernel,
        out_shape=jax.ShapeDtypeStruct((cands, query_rows, width), jnp.bfloat16),
        grid=(cands,),
        in_specs=[
            pl.BlockSpec((query_rows, width), lambda c: (0, 0)),
            pl.BlockSpec(keys.shape, lambda c: (0, 0)),
            pl.BlockSpec(values_t.shape, lambda c: (0, 0)),
            pl.BlockSpec((1, key_rows, HD), lambda c: (c, 0, 0)),
            pl.BlockSpec(bias.T.shape, lambda c: (0, 0)),
        ],
        out_specs=pl.BlockSpec((1, query_rows, width), lambda c: (c, 0, 0)),
        cost_estimate=pl.CostEstimate(
            flops=flops,
            transcendentals=cands * heads * query_rows * key_rows,
            bytes_accessed=window.size * 2 + own_queries.size * 2 + cands * query_rows * width * 2,
        ),
    )(own_queries, keys, values_t, table, bias.T)


def place_kernel(in_ref, out_ref):
    out_ref[...] = in_ref[0]


def side_by_side(blocks):
    count, rows, width = blocks.shape
    return pl.pallas_call(
        place_kernel,
        out_shape=jax.ShapeDtypeStruct((rows, count * width), blocks.dtype),
        grid=(count,),
        in_specs=[pl.BlockSpec((1, rows, width), lambda g: (g, 0, 0))],
        out_specs=pl.BlockSpec((rows, width), lambda g: (0, g)),
    )(blocks)


def cyclic_shift(value, axis, steps):
    count = lax.axis_size(axis)
    return lax.ppermute(value, axis, [(source, (source + steps) % count) for source in range(count)])


def on_device(queries, keys_values, factors, lengths):
    row_count = queries.shape[0]
    group_width = queries.shape[1] // KVH
    device = lax.axis_index("doc")
    group = lax.axis_index("cand")
    query_index = device * row_count + jnp.arange(row_count, dtype=jnp.int32)
    key_index = (device - SPAN) * row_count + jnp.arange((SPAN + 1) * row_count, dtype=jnp.int32)
    cands = lax.axis_size("cand")
    every_factor = lax.all_to_all(
        jnp.broadcast_to(factors, (cands, factors.shape[1])), "cand", 0, 0, tiled=True
    )
    far = passed_along(keys_values, "doc", SPAN)
    window = keys_values
    reach = 1
    while reach < SPAN:
        window = jnp.concatenate([passed_along(window, "doc", reach), window], axis=1)
        reach *= 2
    window = jnp.concatenate([far, window], axis=1)
    query_doc, _ = locate(query_index, lengths)
    key_doc, key_offset = locate(key_index, lengths)
    allowed = (
        (key_doc[None, :] == query_doc[:, None])
        & (key_index[None, :] <= query_index[:, None])
        & (key_doc[None, :] >= 0)
    )
    bias = jnp.where(allowed, 0.0, -1e30).astype(jnp.float32)
    offsets = jnp.broadcast_to(key_offset.astype(jnp.float32)[:, None], (key_offset.shape[0], HD))
    own_queries = lax.dynamic_slice_in_dim(queries, group * group_width, group_width, 1)
    mixed = attend_all(own_queries, window, offsets, inverse_rows(every_factor), bias)
    gathered = lax.all_to_all(mixed, "cand", 0, 0, tiled=True)
    return side_by_side(gathered)[None]


def solution(mesh):
    placed = (P("doc", None), P(None, "doc", "cand"), P("cand", None), P())
    return jax.shard_map(
        on_device, mesh=mesh, in_specs=placed, out_specs=P("cand", "doc", None), check_vma=False
    )
```

```python
import math

import jax
import jax.numpy as jnp
from jax import lax
from jax.experimental import pallas as pl
from jax.experimental.pallas import tpu as pltpu
from jax.sharding import PartitionSpec as P

H = 64
KVH = 8
HD = 128
SPAN = 8


ROPE_BASE = 500000.0


def passed_along(value, axis, steps):
    count = lax.axis_size(axis)
    first, last = (max(0, -steps), min(count, count - steps))
    return lax.ppermute(value, axis, [(source, source + steps) for source in range(first, last)])


def locate(index_rows, lengths):
    ends = jnp.cumsum(lengths)
    starts = ends - lengths
    docid = jnp.sum((index_rows[:, None] >= ends[None, :]).astype(jnp.int32), axis=1)
    onehot = docid[:, None] == jnp.arange(lengths.shape[0], dtype=jnp.int32)[None, :]
    first_row = jnp.sum(jnp.where(onehot, starts[None, :], 0), axis=1)
    valid = index_rows >= 0
    return (jnp.where(valid, docid, -1), jnp.where(valid, index_rows - first_row, 0))


def inverse_rows(factors):
    half_dim = HD // 2
    inverse = jnp.power(ROPE_BASE, -2.0 * jnp.arange(half_dim, dtype=jnp.float32) / HD) / factors
    return jnp.concatenate([inverse, inverse], axis=-1)[:, None, :]


def cos_and_sin(angle, low):
    turns = jnp.floor(angle * 0.636619772367581343 + 0.5)
    rest = ((angle - turns * 1.5703125) - turns * 4.837512969970703125e-4) - turns * 7.54978995489188216e-8
    square = rest * rest
    sine = rest + rest * square * (-1.6666654611e-1 + square * (8.3321608736e-3 + square * -1.9515295891e-4))
    cosine = 1.0 - 0.5 * square + square * square * (
        4.166664568298827e-2 + square * (-1.388731625493765e-3 + square * 2.443315711809948e-5)
    )
    quadrant = turns.astype(jnp.int32) + jnp.where(low, 0, 3)
    base = jnp.where((quadrant & 1) == 1, sine, cosine)
    return jnp.where(((quadrant + 1) & 2) != 0, -base, base)


def attention_kernel(q_ref, k_ref, vt_ref, table_ref, bias_ref, out_ref):
    half_dim = HD // 2
    group_size = H // KVH
    query_rows = q_ref.shape[0]
    table = table_ref[0]
    low = lax.broadcasted_iota(jnp.int32, table.shape, 1) < half_dim
    swapped = pltpu.roll(table, half_dim, 1)
    cosine = jnp.where(low, table, swapped)
    sine = jnp.where(low, -swapped, table)
    keys = k_ref[...].astype(jnp.float32)
    key_rot = (keys * cosine + pltpu.roll(keys, half_dim, 1) * sine).astype(jnp.bfloat16)
    first_query = table.shape[0] - query_rows
    q_cos = cosine[first_query:]
    q_sin = sine[first_query:]
    bias = bias_ref[...]
    scale = 1.0 / math.sqrt(HD)
    stacked = jnp.concatenate(
        [
            (
                q_ref[:, head * HD : (head + 1) * HD].astype(jnp.float32) * q_cos
                + pltpu.roll(q_ref[:, head * HD : (head + 1) * HD].astype(jnp.float32), half_dim, 1) * q_sin
            ).astype(jnp.bfloat16)
            for head in range(group_size)
        ],
        axis=0,
    )
    scores = lax.dot_general(
        key_rot, stacked, (((1,), (1,)), ((), ())), preferred_element_type=jnp.float32
    )
    weights = []
    totals = []
    for head in range(group_size):
        part = scores[:, head * query_rows : (head + 1) * query_rows] * scale + bias
        largest = jnp.max(part, axis=0, keepdims=True)
        expw = jnp.exp(part - largest)
        totals.append(jnp.sum(expw, axis=0, keepdims=True))
        weights.append(expw.astype(jnp.bfloat16))
    numer = jnp.dot(vt_ref[...], jnp.concatenate(weights, axis=1), preferred_element_type=jnp.float32)
    for head in range(group_size):
        cols = numer[:, head * query_rows : (head + 1) * query_rows] / totals[head]
        out_ref[0, :, head * HD : (head + 1) * HD] = cols.T.astype(jnp.bfloat16)


def attend_all(own_queries, window, offsets, inverse, bias):
    angle = offsets[None] * inverse
    low = lax.broadcasted_iota(jnp.int32, angle.shape, 2) < HD // 2
    table = cos_and_sin(angle, low)
    keys = window[0]
    values_t = window[1].T
    cands = inverse.shape[0]
    key_rows = window.shape[1]
    query_rows, width = own_queries.shape
    heads = width // HD
    flops = cands * heads * 4 * query_rows * key_rows * HD
    return pl.pallas_call(
        attention_kernel,
        out_shape=jax.ShapeDtypeStruct((cands, query_rows, width), jnp.bfloat16),
        grid=(cands,),
        in_specs=[
            pl.BlockSpec((query_rows, width), lambda c: (0, 0)),
            pl.BlockSpec(keys.shape, lambda c: (0, 0)),
            pl.BlockSpec(values_t.shape, lambda c: (0, 0)),
            pl.BlockSpec((1, key_rows, HD), lambda c: (c, 0, 0)),
            pl.BlockSpec(bias.T.shape, lambda c: (0, 0)),
        ],
        out_specs=pl.BlockSpec((1, query_rows, width), lambda c: (c, 0, 0)),
        cost_estimate=pl.CostEstimate(
            flops=flops,
            transcendentals=cands * heads * query_rows * key_rows,
            bytes_accessed=window.size * 2 + own_queries.size * 2 + cands * query_rows * width * 2,
        ),
    )(own_queries, keys, values_t, table, bias.T)


def place_kernel(in_ref, out_ref):
    count, _, width = in_ref.shape
    for g in range(count):
        out_ref[:, g * width : (g + 1) * width] = in_ref[g]


def side_by_side(blocks):
    count, rows, width = blocks.shape
    step = count // 2
    return pl.pallas_call(
        place_kernel,
        out_shape=jax.ShapeDtypeStruct((rows, count * width), blocks.dtype),
        grid=(count // step,),
        in_specs=[pl.BlockSpec((step, rows, width), lambda g: (g, 0, 0))],
        out_specs=pl.BlockSpec((rows, step * width), lambda g: (0, g)),
    )(blocks)


def cyclic_shift(value, axis, steps):
    count = lax.axis_size(axis)
    return lax.ppermute(value, axis, [(source, (source + steps) % count) for source in range(count)])


def on_device(queries, keys_values, factors, lengths):
    row_count = queries.shape[0]
    group_width = queries.shape[1] // KVH
    device = lax.axis_index("doc")
    group = lax.axis_index("cand")
    query_index = device * row_count + jnp.arange(row_count, dtype=jnp.int32)
    key_index = (device - SPAN) * row_count + jnp.arange((SPAN + 1) * row_count, dtype=jnp.int32)
    cands = lax.axis_size("cand")
    every_factor = lax.all_to_all(
        jnp.broadcast_to(factors, (cands, factors.shape[1])), "cand", 0, 0, tiled=True
    )
    far = passed_along(keys_values, "doc", SPAN)
    window = keys_values
    reach = 1
    while reach < SPAN:
        window = jnp.concatenate([passed_along(window, "doc", reach), window], axis=1)
        reach *= 2
    window = jnp.concatenate([far, window], axis=1)
    query_doc, _ = locate(query_index, lengths)
    key_doc, key_offset = locate(key_index, lengths)
    allowed = (
        (key_doc[None, :] == query_doc[:, None])
        & (key_index[None, :] <= query_index[:, None])
        & (key_doc[None, :] >= 0)
    )
    bias = jnp.where(allowed, 0.0, -1e30).astype(jnp.float32)
    offsets = jnp.broadcast_to(key_offset.astype(jnp.float32)[:, None], (key_offset.shape[0], HD))
    own_queries = lax.dynamic_slice_in_dim(queries, group * group_width, group_width, 1)
    mixed = attend_all(own_queries, window, offsets, inverse_rows(every_factor), bias)
    gathered = lax.all_to_all(mixed, "cand", 0, 0, tiled=True)
    return side_by_side(gathered)[None]


def solution(mesh):
    placed = (P("doc", None), P(None, "doc", "cand"), P("cand", None), P())
    return jax.shard_map(
        on_device, mesh=mesh, in_specs=placed, out_specs=P("cand", "doc", None), check_vma=False
    )
```

```python
import math

import jax
import jax.numpy as jnp
from jax import lax
from jax.experimental import pallas as pl
from jax.experimental.pallas import tpu as pltpu
from jax.sharding import Mesh, PartitionSpec as P

H = 64
KVH = 8
HD = 128
SPAN = 8
CAND = ("chip", "core")


ROPE_BASE = 500000.0


def passed_along(value, axis, steps):
    count = lax.axis_size(axis)
    first, last = (max(0, -steps), min(count, count - steps))
    return lax.ppermute(value, axis, [(source, source + steps) for source in range(first, last)])


def locate(index_rows, lengths):
    ends = jnp.cumsum(lengths)
    starts = ends - lengths
    docid = jnp.sum((index_rows[:, None] >= ends[None, :]).astype(jnp.int32), axis=1)
    onehot = docid[:, None] == jnp.arange(lengths.shape[0], dtype=jnp.int32)[None, :]
    first_row = jnp.sum(jnp.where(onehot, starts[None, :], 0), axis=1)
    valid = index_rows >= 0
    return (jnp.where(valid, docid, -1), jnp.where(valid, index_rows - first_row, 0))


def inverse_rows(factors):
    half_dim = HD // 2
    inverse = jnp.power(ROPE_BASE, -2.0 * jnp.arange(half_dim, dtype=jnp.float32) / HD) / factors
    return jnp.concatenate([inverse, inverse], axis=-1)[:, None, :]


def cos_and_sin(angle, low):
    turns = jnp.floor(angle * 0.636619772367581343 + 0.5)
    rest = ((angle - turns * 1.5703125) - turns * 4.837512969970703125e-4) - turns * 7.54978995489188216e-8
    square = rest * rest
    sine = rest + rest * square * (-1.6666654611e-1 + square * (8.3321608736e-3 + square * -1.9515295891e-4))
    cosine = 1.0 - 0.5 * square + square * square * (
        4.166664568298827e-2 + square * (-1.388731625493765e-3 + square * 2.443315711809948e-5)
    )
    quadrant = turns.astype(jnp.int32) + jnp.where(low, 0, 3)
    base = jnp.where((quadrant & 1) == 1, sine, cosine)
    return jnp.where(((quadrant + 1) & 2) != 0, -base, base)


def attention_kernel(q_ref, k_ref, vt_ref, table_ref, bias_ref, out_ref):
    half_dim = HD // 2
    group_size = H // KVH
    query_rows = q_ref.shape[0]
    table = table_ref[0]
    low = lax.broadcasted_iota(jnp.int32, table.shape, 1) < half_dim
    swapped = pltpu.roll(table, half_dim, 1)
    cosine = jnp.where(low, table, swapped)
    sine = jnp.where(low, -swapped, table)
    keys = k_ref[...].astype(jnp.float32)
    key_rot = (keys * cosine + pltpu.roll(keys, half_dim, 1) * sine).astype(jnp.bfloat16)
    first_query = table.shape[0] - query_rows
    q_cos = cosine[first_query:]
    q_sin = sine[first_query:]
    bias = bias_ref[...]
    scale = 1.0 / math.sqrt(HD)
    stacked = jnp.concatenate(
        [
            (
                q_ref[:, head * HD : (head + 1) * HD].astype(jnp.float32) * q_cos
                + pltpu.roll(q_ref[:, head * HD : (head + 1) * HD].astype(jnp.float32), half_dim, 1) * q_sin
            ).astype(jnp.bfloat16)
            for head in range(group_size)
        ],
        axis=0,
    )
    scores = lax.dot_general(
        key_rot, stacked, (((1,), (1,)), ((), ())), preferred_element_type=jnp.float32
    )
    weights = []
    totals = []
    for head in range(group_size):
        part = scores[:, head * query_rows : (head + 1) * query_rows] * scale + bias
        largest = jnp.max(part, axis=0, keepdims=True)
        expw = jnp.exp(part - largest)
        totals.append(jnp.sum(expw, axis=0, keepdims=True))
        weights.append(expw.astype(jnp.bfloat16))
    numer = jnp.dot(vt_ref[...], jnp.concatenate(weights, axis=1), preferred_element_type=jnp.float32)
    for head in range(group_size):
        cols = numer[:, head * query_rows : (head + 1) * query_rows] / totals[head]
        out_ref[0, :, head * HD : (head + 1) * HD] = cols.T.astype(jnp.bfloat16)


def attend_all(own_queries, window, offsets, inverse, bias):
    angle = offsets[None] * inverse
    low = lax.broadcasted_iota(jnp.int32, angle.shape, 2) < HD // 2
    table = cos_and_sin(angle, low)
    keys = window[0]
    values_t = window[1].T
    cands = inverse.shape[0]
    key_rows = window.shape[1]
    query_rows, width = own_queries.shape
    heads = width // HD
    flops = cands * heads * 4 * query_rows * key_rows * HD
    return pl.pallas_call(
        attention_kernel,
        out_shape=jax.ShapeDtypeStruct((cands, query_rows, width), jnp.bfloat16),
        grid=(cands,),
        in_specs=[
            pl.BlockSpec((query_rows, width), lambda c: (0, 0)),
            pl.BlockSpec(keys.shape, lambda c: (0, 0)),
            pl.BlockSpec(values_t.shape, lambda c: (0, 0)),
            pl.BlockSpec((1, key_rows, HD), lambda c: (c, 0, 0)),
            pl.BlockSpec(bias.T.shape, lambda c: (0, 0)),
        ],
        out_specs=pl.BlockSpec((1, query_rows, width), lambda c: (c, 0, 0)),
        cost_estimate=pl.CostEstimate(
            flops=flops,
            transcendentals=cands * heads * query_rows * key_rows,
            bytes_accessed=window.size * 2 + own_queries.size * 2 + cands * query_rows * width * 2,
        ),
    )(own_queries, keys, values_t, table, bias.T)


def place_kernel(in_ref, out_ref):
    count, _, width = in_ref.shape
    for g in range(count):
        out_ref[:, g * width : (g + 1) * width] = in_ref[g]


def side_by_side(blocks):
    count, rows, width = blocks.shape
    step = count // 2
    return pl.pallas_call(
        place_kernel,
        out_shape=jax.ShapeDtypeStruct((rows, count * width), blocks.dtype),
        grid=(count // step,),
        in_specs=[pl.BlockSpec((step, rows, width), lambda g: (g, 0, 0))],
        out_specs=pl.BlockSpec((rows, step * width), lambda g: (0, g)),
    )(blocks)


def cyclic_shift(value, axis, steps):
    count = lax.axis_size(axis)
    return lax.ppermute(value, axis, [(source, (source + steps) % count) for source in range(count)])


def on_device(queries, keys_values, factors, lengths):
    row_count = queries.shape[0]
    group_width = queries.shape[1] // KVH
    device = lax.axis_index("doc")
    group = lax.axis_index(CAND)
    query_index = device * row_count + jnp.arange(row_count, dtype=jnp.int32)
    key_index = (device - SPAN) * row_count + jnp.arange((SPAN + 1) * row_count, dtype=jnp.int32)
    cands = lax.axis_size(CAND)
    every_factor = lax.all_to_all(
        jnp.broadcast_to(factors, (cands, factors.shape[1])), CAND, 0, 0, tiled=True
    )
    far = passed_along(keys_values, "doc", SPAN)
    window = keys_values
    reach = 1
    while reach < SPAN:
        window = jnp.concatenate([passed_along(window, "doc", reach), window], axis=1)
        reach *= 2
    window = jnp.concatenate([far, window], axis=1)
    query_doc, _ = locate(query_index, lengths)
    key_doc, key_offset = locate(key_index, lengths)
    allowed = (
        (key_doc[None, :] == query_doc[:, None])
        & (key_index[None, :] <= query_index[:, None])
        & (key_doc[None, :] >= 0)
    )
    bias = jnp.where(allowed, 0.0, -1e30).astype(jnp.float32)
    offsets = jnp.broadcast_to(key_offset.astype(jnp.float32)[:, None], (key_offset.shape[0], HD))
    own_queries = lax.dynamic_slice_in_dim(queries, group * group_width, group_width, 1)
    cores = lax.axis_size("core")
    chips = cands // cores
    order = [chip * cores + core for core in range(cores) for chip in range(chips)]
    mixed = attend_all(own_queries, window, offsets, inverse_rows(every_factor[jnp.array(order)]), bias)
    mixed = mixed.reshape(cores, chips, row_count, group_width)
    paired = lax.all_to_all(mixed, "core", 0, 0, tiled=True)
    gathered = lax.all_to_all(paired, "chip", 1, 0, tiled=True)
    return side_by_side(gathered.reshape(cands, row_count, group_width))[None]


def solution(mesh):
    cand = mesh.shape["cand"]
    split = Mesh(mesh.devices.reshape(cand // 2, 2, mesh.shape["doc"]), ("chip", "core", "doc"))
    placed = (P("doc", None), P(None, "doc", CAND), P(CAND, None), P())
    return jax.shard_map(
        on_device, mesh=split, in_specs=placed, out_specs=P(CAND, "doc", None), check_vma=False
    )
```

```python
import math

import jax
import jax.numpy as jnp
from jax import lax
from jax.experimental import pallas as pl
from jax.experimental.pallas import tpu as pltpu
from jax.sharding import PartitionSpec as P

H = 64
KVH = 8
HD = 128
SPAN = 8


ROPE_BASE = 500000.0


def passed_along(value, axis, steps):
    count = lax.axis_size(axis)
    first, last = (max(0, -steps), min(count, count - steps))
    return lax.ppermute(value, axis, [(source, source + steps) for source in range(first, last)])


def locate(index_rows, lengths):
    ends = jnp.cumsum(lengths)
    starts = ends - lengths
    docid = jnp.sum((index_rows[:, None] >= ends[None, :]).astype(jnp.int32), axis=1)
    onehot = docid[:, None] == jnp.arange(lengths.shape[0], dtype=jnp.int32)[None, :]
    first_row = jnp.sum(jnp.where(onehot, starts[None, :], 0), axis=1)
    valid = index_rows >= 0
    return (jnp.where(valid, docid, -1), jnp.where(valid, index_rows - first_row, 0))


def inverse_rows(factors):
    half_dim = HD // 2
    inverse = jnp.power(ROPE_BASE, -2.0 * jnp.arange(half_dim, dtype=jnp.float32) / HD) / factors
    return jnp.concatenate([inverse, inverse], axis=-1)[:, None, :]


def cos_and_sin(angle, low):
    turns = jnp.floor(angle * 0.636619772367581343 + 0.5)
    rest = ((angle - turns * 1.5703125) - turns * 4.837512969970703125e-4) - turns * 7.54978995489188216e-8
    square = rest * rest
    sine = rest + rest * square * (-1.6666654611e-1 + square * (8.3321608736e-3 + square * -1.9515295891e-4))
    cosine = 1.0 - 0.5 * square + square * square * (
        4.166664568298827e-2 + square * (-1.388731625493765e-3 + square * 2.443315711809948e-5)
    )
    quadrant = turns.astype(jnp.int32) + jnp.where(low, 0, 3)
    base = jnp.where((quadrant & 1) == 1, sine, cosine)
    return jnp.where(((quadrant + 1) & 2) != 0, -base, base)


def attention_kernel(q_ref, kv_ref, table_ref, bias_ref, out_ref):
    half_dim = HD // 2
    group_size = H // KVH
    query_rows = q_ref.shape[0]
    table = table_ref[0]
    low = lax.broadcasted_iota(jnp.int32, table.shape, 1) < half_dim
    swapped = pltpu.roll(table, half_dim, 1)
    cosine = jnp.where(low, table, swapped)
    sine = jnp.where(low, -swapped, table)
    keys = kv_ref[0].astype(jnp.float32)
    key_rot = (keys * cosine + pltpu.roll(keys, half_dim, 1) * sine).astype(jnp.bfloat16)
    first_query = table.shape[0] - query_rows
    q_cos = cosine[first_query:]
    q_sin = sine[first_query:]
    bias = bias_ref[...]
    scale = 1.0 / math.sqrt(HD)
    stacked = jnp.concatenate(
        [
            (
                q_ref[:, head * HD : (head + 1) * HD].astype(jnp.float32) * q_cos
                + pltpu.roll(q_ref[:, head * HD : (head + 1) * HD].astype(jnp.float32), half_dim, 1) * q_sin
            ).astype(jnp.bfloat16)
            for head in range(group_size)
        ],
        axis=0,
    )
    scores = lax.dot_general(
        key_rot, stacked, (((1,), (1,)), ((), ())), preferred_element_type=jnp.float32
    )
    weights = []
    totals = []
    for head in range(group_size):
        part = scores[:, head * query_rows : (head + 1) * query_rows] * scale + bias
        largest = jnp.max(part, axis=0, keepdims=True)
        expw = jnp.exp(part - largest)
        totals.append(jnp.sum(expw, axis=0, keepdims=True))
        weights.append(expw.astype(jnp.bfloat16))
    numer = lax.dot_general(
        kv_ref[1], jnp.concatenate(weights, axis=1), (((0,), (0,)), ((), ())),
        preferred_element_type=jnp.float32,
    )
    for head in range(group_size):
        cols = numer[:, head * query_rows : (head + 1) * query_rows] / totals[head]
        out_ref[0, :, head * HD : (head + 1) * HD] = cols.T.astype(jnp.bfloat16)


def attend_all(own_queries, window, offsets, inverse, bias):
    angle = offsets[None] * inverse
    low = lax.broadcasted_iota(jnp.int32, angle.shape, 2) < HD // 2
    table = cos_and_sin(angle, low)
    cands = inverse.shape[0]
    key_rows = window.shape[1]
    query_rows, width = own_queries.shape
    heads = width // HD
    flops = cands * heads * 4 * query_rows * key_rows * HD
    return pl.pallas_call(
        attention_kernel,
        out_shape=jax.ShapeDtypeStruct((cands, query_rows, width), jnp.bfloat16),
        grid=(cands,),
        in_specs=[
            pl.BlockSpec((query_rows, width), lambda c: (0, 0)),
            pl.BlockSpec(window.shape, lambda c: (0, 0, 0)),
            pl.BlockSpec((1, key_rows, HD), lambda c: (c, 0, 0)),
            pl.BlockSpec(bias.T.shape, lambda c: (0, 0)),
        ],
        out_specs=pl.BlockSpec((1, query_rows, width), lambda c: (c, 0, 0)),
        cost_estimate=pl.CostEstimate(
            flops=flops,
            transcendentals=cands * heads * query_rows * key_rows,
            bytes_accessed=window.size * 2 + own_queries.size * 2 + cands * query_rows * width * 2,
        ),
    )(own_queries, window, table, bias.T)


def place_kernel(in_ref, out_ref):
    count, _, width = in_ref.shape
    for g in range(count):
        out_ref[:, g * width : (g + 1) * width] = in_ref[g]


def side_by_side(blocks):
    count, rows, width = blocks.shape
    step = count // 2
    return pl.pallas_call(
        place_kernel,
        out_shape=jax.ShapeDtypeStruct((rows, count * width), blocks.dtype),
        grid=(count // step,),
        in_specs=[pl.BlockSpec((step, rows, width), lambda g: (g, 0, 0))],
        out_specs=pl.BlockSpec((rows, step * width), lambda g: (0, g)),
    )(blocks)


def cyclic_shift(value, axis, steps):
    count = lax.axis_size(axis)
    return lax.ppermute(value, axis, [(source, (source + steps) % count) for source in range(count)])


def on_device(queries, keys_values, factors, lengths):
    row_count = queries.shape[0]
    group_width = queries.shape[1] // KVH
    device = lax.axis_index("doc")
    group = lax.axis_index("cand")
    query_index = device * row_count + jnp.arange(row_count, dtype=jnp.int32)
    key_index = (device - SPAN) * row_count + jnp.arange((SPAN + 1) * row_count, dtype=jnp.int32)
    cands = lax.axis_size("cand")
    every_factor = lax.all_to_all(
        jnp.broadcast_to(factors, (cands, factors.shape[1])), "cand", 0, 0, tiled=True
    )
    far = passed_along(keys_values, "doc", SPAN)
    window = keys_values
    reach = 1
    while reach < SPAN:
        window = jnp.concatenate([passed_along(window, "doc", reach), window], axis=1)
        reach *= 2
    window = jnp.concatenate([far, window], axis=1)
    query_doc, _ = locate(query_index, lengths)
    key_doc, key_offset = locate(key_index, lengths)
    allowed = (
        (key_doc[None, :] == query_doc[:, None])
        & (key_index[None, :] <= query_index[:, None])
        & (key_doc[None, :] >= 0)
    )
    bias = jnp.where(allowed, 0.0, -1e30).astype(jnp.float32)
    offsets = jnp.broadcast_to(key_offset.astype(jnp.float32)[:, None], (key_offset.shape[0], HD))
    own_queries = lax.dynamic_slice_in_dim(queries, group * group_width, group_width, 1)
    mixed = attend_all(own_queries, window, offsets, inverse_rows(every_factor), bias)
    gathered = lax.all_to_all(mixed, "cand", 0, 0, tiled=True)
    return side_by_side(gathered)[None]


def solution(mesh):
    placed = (P("doc", None), P(None, "doc", "cand"), P("cand", None), P())
    return jax.shard_map(
        on_device, mesh=mesh, in_specs=placed, out_specs=P("cand", "doc", None), check_vma=False
    )
```

```python
import math

import jax
import jax.numpy as jnp
from jax import lax
from jax.experimental import pallas as pl
from jax.experimental.pallas import tpu as pltpu
from jax.sharding import PartitionSpec as P

H = 64
KVH = 8
HD = 128
SPAN = 8


ROPE_BASE = 500000.0


def passed_along(value, axis, steps):
    count = lax.axis_size(axis)
    first, last = (max(0, -steps), min(count, count - steps))
    return lax.ppermute(value, axis, [(source, source + steps) for source in range(first, last)])


def locate(index_rows, lengths):
    ends = jnp.cumsum(lengths)
    starts = ends - lengths
    docid = jnp.sum((index_rows[:, None] >= ends[None, :]).astype(jnp.int32), axis=1)
    onehot = docid[:, None] == jnp.arange(lengths.shape[0], dtype=jnp.int32)[None, :]
    first_row = jnp.sum(jnp.where(onehot, starts[None, :], 0), axis=1)
    valid = index_rows >= 0
    return (jnp.where(valid, docid, -1), jnp.where(valid, index_rows - first_row, 0))


def inverse_rows(factors):
    half_dim = HD // 2
    inverse = jnp.power(ROPE_BASE, -2.0 * jnp.arange(half_dim, dtype=jnp.float32) / HD) / factors
    return jnp.concatenate([inverse, inverse], axis=-1)[:, None, :]


def cos_and_sin(angle, low):
    turns = jnp.floor(angle * 0.636619772367581343 + 0.5)
    rest = ((angle - turns * 1.5703125) - turns * 4.837512969970703125e-4) - turns * 7.54978995489188216e-8
    square = rest * rest
    sine = rest + rest * square * (-1.6666654611e-1 + square * (8.3321608736e-3 + square * -1.9515295891e-4))
    cosine = 1.0 - 0.5 * square + square * square * (
        4.166664568298827e-2 + square * (-1.388731625493765e-3 + square * 2.443315711809948e-5)
    )
    quadrant = turns.astype(jnp.int32) + jnp.where(low, 0, 3)
    base = jnp.where((quadrant & 1) == 1, sine, cosine)
    return jnp.where(((quadrant + 1) & 2) != 0, -base, base)


def attention_kernel(q_ref, kv_ref, table_ref, bias_ref, out_ref):
    half_dim = HD // 2
    group_size = H // KVH
    query_rows = q_ref.shape[0]
    table = table_ref[0]
    low = lax.broadcasted_iota(jnp.int32, table.shape, 1) < half_dim
    swapped = pltpu.roll(table, half_dim, 1)
    cosine = jnp.where(low, table, swapped)
    sine = jnp.where(low, -swapped, table)
    keys = kv_ref[0].astype(jnp.float32)
    key_rot = (keys * cosine + pltpu.roll(keys, half_dim, 1) * sine).astype(jnp.bfloat16)
    first_query = table.shape[0] - query_rows
    q_cos = cosine[first_query:]
    q_sin = sine[first_query:]
    bias = bias_ref[...]
    scale = 1.0 / math.sqrt(HD)
    stacked = jnp.concatenate(
        [
            (
                q_ref[:, head * HD : (head + 1) * HD].astype(jnp.float32) * q_cos
                + pltpu.roll(q_ref[:, head * HD : (head + 1) * HD].astype(jnp.float32), half_dim, 1) * q_sin
            ).astype(jnp.bfloat16)
            for head in range(group_size)
        ],
        axis=0,
    )
    scores = lax.dot_general(
        key_rot, stacked, (((1,), (1,)), ((), ())), preferred_element_type=jnp.float32
    )
    weights = []
    totals = []
    for head in range(group_size):
        part = scores[:, head * query_rows : (head + 1) * query_rows] * scale + bias
        largest = jnp.max(part, axis=0, keepdims=True)
        expw = jnp.exp(part - largest)
        totals.append(jnp.sum(expw, axis=0, keepdims=True))
        weights.append(expw.astype(jnp.bfloat16))
    numer = lax.dot_general(
        kv_ref[1], jnp.concatenate(weights, axis=1), (((0,), (0,)), ((), ())),
        preferred_element_type=jnp.float32,
    )
    for head in range(group_size):
        cols = numer[:, head * query_rows : (head + 1) * query_rows] / totals[head]
        out_ref[0, :, head * HD : (head + 1) * HD] = cols.T.astype(jnp.bfloat16)


def attend_all(own_queries, window, offsets, inverse, bias):
    angle = offsets[None] * inverse
    low = lax.broadcasted_iota(jnp.int32, angle.shape, 2) < HD // 2
    table = cos_and_sin(angle, low)
    cands = inverse.shape[0]
    key_rows = window.shape[1]
    query_rows, width = own_queries.shape
    heads = width // HD
    flops = cands * heads * 4 * query_rows * key_rows * HD
    return pl.pallas_call(
        attention_kernel,
        out_shape=jax.ShapeDtypeStruct((cands, query_rows, width), jnp.bfloat16),
        grid=(cands,),
        in_specs=[
            pl.BlockSpec((query_rows, width), lambda c: (0, 0)),
            pl.BlockSpec(window.shape, lambda c: (0, 0, 0)),
            pl.BlockSpec((1, key_rows, HD), lambda c: (c, 0, 0)),
            pl.BlockSpec(bias.T.shape, lambda c: (0, 0)),
        ],
        out_specs=pl.BlockSpec((1, query_rows, width), lambda c: (c, 0, 0)),
        cost_estimate=pl.CostEstimate(
            flops=flops,
            transcendentals=cands * heads * query_rows * key_rows,
            bytes_accessed=window.size * 2 + own_queries.size * 2 + cands * query_rows * width * 2,
        ),
    )(own_queries, window, table, bias.T)


def place_kernel(in_ref, out_ref):
    count, _, width = in_ref.shape
    for g in range(count):
        out_ref[:, g * width : (g + 1) * width] = in_ref[g]


def side_by_side(blocks):
    count, rows, width = blocks.shape
    step = count // 2
    return pl.pallas_call(
        place_kernel,
        out_shape=jax.ShapeDtypeStruct((rows, count * width), blocks.dtype),
        grid=(count // step,),
        in_specs=[pl.BlockSpec((step, rows, width), lambda g: (g, 0, 0))],
        out_specs=pl.BlockSpec((rows, step * width), lambda g: (0, g)),
    )(blocks)


def cyclic_shift(value, axis, steps):
    count = lax.axis_size(axis)
    return lax.ppermute(value, axis, [(source, (source + steps) % count) for source in range(count)])


def on_device(queries, keys_values, factors, lengths):
    row_count = queries.shape[0]
    group_width = queries.shape[1] // KVH
    device = lax.axis_index("doc")
    group = lax.axis_index("cand")
    query_index = device * row_count + jnp.arange(row_count, dtype=jnp.int32)
    key_index = (device - SPAN) * row_count + jnp.arange((SPAN + 1) * row_count, dtype=jnp.int32)
    far = passed_along(keys_values, "doc", SPAN)
    window = keys_values
    reach = 1
    while reach < SPAN:
        window = jnp.concatenate([passed_along(window, "doc", reach), window], axis=1)
        if reach == 1:
            window, factors, lengths, queries = lax.optimization_barrier(
                (window, factors, lengths, queries)
            )
        reach *= 2
    window = jnp.concatenate([far, window], axis=1)
    cands = lax.axis_size("cand")
    every_factor = lax.all_to_all(
        jnp.broadcast_to(factors, (cands, factors.shape[1])), "cand", 0, 0, tiled=True
    )
    query_doc, _ = locate(query_index, lengths)
    key_doc, key_offset = locate(key_index, lengths)
    allowed = (
        (key_doc[None, :] == query_doc[:, None])
        & (key_index[None, :] <= query_index[:, None])
        & (key_doc[None, :] >= 0)
    )
    bias = jnp.where(allowed, 0.0, -1e30).astype(jnp.float32)
    offsets = jnp.broadcast_to(key_offset.astype(jnp.float32)[:, None], (key_offset.shape[0], HD))
    own_queries = lax.dynamic_slice_in_dim(queries, group * group_width, group_width, 1)
    mixed = attend_all(own_queries, window, offsets, inverse_rows(every_factor), bias)
    gathered = lax.all_to_all(mixed, "cand", 0, 0, tiled=True)
    return side_by_side(gathered)[None]


def solution(mesh):
    placed = (P("doc", None), P(None, "doc", "cand"), P("cand", None), P())
    return jax.shard_map(
        on_device, mesh=mesh, in_specs=placed, out_specs=P("cand", "doc", None), check_vma=False
    )
```

```python
import math

import jax
import jax.numpy as jnp
from jax import lax
from jax.experimental import pallas as pl
from jax.experimental.pallas import tpu as pltpu
from jax.sharding import PartitionSpec as P

H = 64
KVH = 8
HD = 128
SPAN = 8


ROPE_BASE = 500000.0


def passed_along(value, axis, steps):
    count = lax.axis_size(axis)
    first, last = (max(0, -steps), min(count, count - steps))
    return lax.ppermute(value, axis, [(source, source + steps) for source in range(first, last)])


def locate(index_rows, lengths):
    ends = jnp.cumsum(lengths)
    starts = ends - lengths
    docid = jnp.sum((index_rows[:, None] >= ends[None, :]).astype(jnp.int32), axis=1)
    onehot = docid[:, None] == jnp.arange(lengths.shape[0], dtype=jnp.int32)[None, :]
    first_row = jnp.sum(jnp.where(onehot, starts[None, :], 0), axis=1)
    valid = index_rows >= 0
    return (jnp.where(valid, docid, -1), jnp.where(valid, index_rows - first_row, 0))


def inverse_rows(factors):
    half_dim = HD // 2
    inverse = jnp.power(ROPE_BASE, -2.0 * jnp.arange(half_dim, dtype=jnp.float32) / HD) / factors
    return jnp.concatenate([inverse, inverse], axis=-1)[:, None, :]


def cos_and_sin(angle, low):
    turns = jnp.floor(angle * 0.636619772367581343 + 0.5)
    rest = ((angle - turns * 1.5703125) - turns * 4.837512969970703125e-4) - turns * 7.54978995489188216e-8
    square = rest * rest
    sine = rest + rest * square * (-1.6666654611e-1 + square * (8.3321608736e-3 + square * -1.9515295891e-4))
    cosine = 1.0 - 0.5 * square + square * square * (
        4.166664568298827e-2 + square * (-1.388731625493765e-3 + square * 2.443315711809948e-5)
    )
    quadrant = turns.astype(jnp.int32) + jnp.where(low, 0, 3)
    base = jnp.where((quadrant & 1) == 1, sine, cosine)
    return jnp.where(((quadrant + 1) & 2) != 0, -base, base)


def attention_kernel(q_ref, kv_ref, table_ref, bias_ref, out_ref):
    half_dim = HD // 2
    group_size = H // KVH
    query_rows = q_ref.shape[0]
    table = table_ref[0]
    low = lax.broadcasted_iota(jnp.int32, table.shape, 1) < half_dim
    swapped = pltpu.roll(table, half_dim, 1)
    cosine = jnp.where(low, table, swapped)
    sine = jnp.where(low, -swapped, table)
    keys = kv_ref[0].astype(jnp.float32)
    key_rot = (keys * cosine + pltpu.roll(keys, half_dim, 1) * sine).astype(jnp.bfloat16)
    first_query = table.shape[0] - query_rows
    q_cos = cosine[first_query:]
    q_sin = sine[first_query:]
    bias = bias_ref[...]
    scale = 1.0 / math.sqrt(HD)
    stacked = jnp.concatenate(
        [
            (
                q_ref[:, head * HD : (head + 1) * HD].astype(jnp.float32) * q_cos
                + pltpu.roll(q_ref[:, head * HD : (head + 1) * HD].astype(jnp.float32), half_dim, 1) * q_sin
            ).astype(jnp.bfloat16)
            for head in range(group_size)
        ],
        axis=0,
    )
    scores = lax.dot_general(
        key_rot, stacked, (((1,), (1,)), ((), ())), preferred_element_type=jnp.float32
    )
    weights = []
    totals = []
    for head in range(group_size):
        part = scores[:, head * query_rows : (head + 1) * query_rows] * scale + bias
        largest = jnp.max(part, axis=0, keepdims=True)
        expw = jnp.exp(part - largest)
        totals.append(jnp.sum(expw, axis=0, keepdims=True))
        weights.append(expw.astype(jnp.bfloat16))
    numer = lax.dot_general(
        kv_ref[1], jnp.concatenate(weights, axis=1), (((0,), (0,)), ((), ())),
        preferred_element_type=jnp.float32,
    )
    for head in range(group_size):
        cols = numer[:, head * query_rows : (head + 1) * query_rows] / totals[head]
        out_ref[0, :, head * HD : (head + 1) * HD] = cols.T.astype(jnp.bfloat16)


def attend_all(own_queries, window, offsets, inverse, bias):
    angle = offsets[None] * inverse
    low = lax.broadcasted_iota(jnp.int32, angle.shape, 2) < HD // 2
    table = cos_and_sin(angle, low)
    cands = inverse.shape[0]
    key_rows = window.shape[1]
    query_rows, width = own_queries.shape
    heads = width // HD
    flops = cands * heads * 4 * query_rows * key_rows * HD
    return pl.pallas_call(
        attention_kernel,
        out_shape=jax.ShapeDtypeStruct((cands, query_rows, width), jnp.bfloat16),
        grid=(cands,),
        in_specs=[
            pl.BlockSpec((query_rows, width), lambda c: (0, 0)),
            pl.BlockSpec(window.shape, lambda c: (0, 0, 0)),
            pl.BlockSpec((1, key_rows, HD), lambda c: (c, 0, 0)),
            pl.BlockSpec(bias.T.shape, lambda c: (0, 0)),
        ],
        out_specs=pl.BlockSpec((1, query_rows, width), lambda c: (c, 0, 0)),
        cost_estimate=pl.CostEstimate(
            flops=flops,
            transcendentals=cands * heads * query_rows * key_rows,
            bytes_accessed=window.size * 2 + own_queries.size * 2 + cands * query_rows * width * 2,
        ),
    )(own_queries, window, table, bias.T)


def place_kernel(in_ref, out_ref):
    count, _, width = in_ref.shape
    for g in range(count):
        out_ref[:, g * width : (g + 1) * width] = in_ref[g]


def side_by_side(blocks):
    count, rows, width = blocks.shape
    step = count // 2
    return pl.pallas_call(
        place_kernel,
        out_shape=jax.ShapeDtypeStruct((rows, count * width), blocks.dtype),
        grid=(count // step,),
        in_specs=[pl.BlockSpec((step, rows, width), lambda g: (g, 0, 0))],
        out_specs=pl.BlockSpec((rows, step * width), lambda g: (0, g)),
    )(blocks)


def cyclic_shift(value, axis, steps):
    count = lax.axis_size(axis)
    return lax.ppermute(value, axis, [(source, (source + steps) % count) for source in range(count)])


def on_device(queries, keys_values, factors, lengths):
    row_count = queries.shape[0]
    group_width = queries.shape[1] // KVH
    device = lax.axis_index("doc")
    group = lax.axis_index("cand")
    query_index = device * row_count + jnp.arange(row_count, dtype=jnp.int32)
    key_index = (device - SPAN) * row_count + jnp.arange((SPAN + 1) * row_count, dtype=jnp.int32)
    far = passed_along(keys_values, "doc", SPAN)
    quarter = SPAN // 2
    near = jnp.concatenate(
        [passed_along(keys_values, "doc", step) for step in range(quarter - 1, 0, -1)] + [keys_values],
        axis=1,
    )
    near, factors, lengths, queries = lax.optimization_barrier((near, factors, lengths, queries))
    window = jnp.concatenate([passed_along(near, "doc", quarter), near], axis=1)
    window = jnp.concatenate([far, window], axis=1)
    cands = lax.axis_size("cand")
    every_factor = lax.all_to_all(
        jnp.broadcast_to(factors, (cands, factors.shape[1])), "cand", 0, 0, tiled=True
    )
    query_doc, _ = locate(query_index, lengths)
    key_doc, key_offset = locate(key_index, lengths)
    allowed = (
        (key_doc[None, :] == query_doc[:, None])
        & (key_index[None, :] <= query_index[:, None])
        & (key_doc[None, :] >= 0)
    )
    bias = jnp.where(allowed, 0.0, -1e30).astype(jnp.float32)
    offsets = jnp.broadcast_to(key_offset.astype(jnp.float32)[:, None], (key_offset.shape[0], HD))
    own_queries = lax.dynamic_slice_in_dim(queries, group * group_width, group_width, 1)
    mixed = attend_all(own_queries, window, offsets, inverse_rows(every_factor), bias)
    gathered = lax.all_to_all(mixed, "cand", 0, 0, tiled=True)
    return side_by_side(gathered)[None]


def solution(mesh):
    placed = (P("doc", None), P(None, "doc", "cand"), P("cand", None), P())
    return jax.shard_map(
        on_device, mesh=mesh, in_specs=placed, out_specs=P("cand", "doc", None), check_vma=False
    )
```

```python
import math

import jax
import jax.numpy as jnp
from jax import lax
from jax.experimental import pallas as pl
from jax.experimental.pallas import tpu as pltpu
from jax.sharding import PartitionSpec as P

H = 64
KVH = 8
HD = 128
SPAN = 8


ROPE_BASE = 500000.0


def passed_along(value, axis, steps):
    count = lax.axis_size(axis)
    first, last = (max(0, -steps), min(count, count - steps))
    return lax.ppermute(value, axis, [(source, source + steps) for source in range(first, last)])


def locate(index_rows, lengths):
    ends = jnp.cumsum(lengths)
    starts = ends - lengths
    docid = jnp.sum((index_rows[:, None] >= ends[None, :]).astype(jnp.int32), axis=1)
    onehot = docid[:, None] == jnp.arange(lengths.shape[0], dtype=jnp.int32)[None, :]
    first_row = jnp.sum(jnp.where(onehot, starts[None, :], 0), axis=1)
    valid = index_rows >= 0
    return (jnp.where(valid, docid, -1), jnp.where(valid, index_rows - first_row, 0))


def inverse_rows(factors):
    half_dim = HD // 2
    inverse = jnp.power(ROPE_BASE, -2.0 * jnp.arange(half_dim, dtype=jnp.float32) / HD) / factors
    return jnp.concatenate([inverse, inverse], axis=-1)[:, None, :]


def cos_and_sin(angle, low):
    turns = jnp.floor(angle * 0.636619772367581343 + 0.5)
    rest = ((angle - turns * 1.5703125) - turns * 4.837512969970703125e-4) - turns * 7.54978995489188216e-8
    square = rest * rest
    sine = rest + rest * square * (-1.6666654611e-1 + square * (8.3321608736e-3 + square * -1.9515295891e-4))
    cosine = 1.0 - 0.5 * square + square * square * (
        4.166664568298827e-2 + square * (-1.388731625493765e-3 + square * 2.443315711809948e-5)
    )
    quadrant = turns.astype(jnp.int32) + jnp.where(low, 0, 3)
    base = jnp.where((quadrant & 1) == 1, sine, cosine)
    return jnp.where(((quadrant + 1) & 2) != 0, -base, base)


def attention_kernel(q_ref, far_ref, mid_ref, near_ref, table_ref, bias_ref, out_ref):
    half_dim = HD // 2
    group_size = H // KVH
    query_rows = q_ref.shape[0]
    table = table_ref[0]
    low = lax.broadcasted_iota(jnp.int32, table.shape, 1) < half_dim
    swapped = pltpu.roll(table, half_dim, 1)
    cosine = jnp.where(low, table, swapped)
    sine = jnp.where(low, -swapped, table)
    keys = jnp.concatenate([far_ref[0], mid_ref[0], near_ref[0]], axis=0).astype(jnp.float32)
    key_rot = (keys * cosine + pltpu.roll(keys, half_dim, 1) * sine).astype(jnp.bfloat16)
    first_query = table.shape[0] - query_rows
    q_cos = cosine[first_query:]
    q_sin = sine[first_query:]
    bias = bias_ref[...]
    scale = 1.0 / math.sqrt(HD)
    stacked = jnp.concatenate(
        [
            (
                q_ref[:, head * HD : (head + 1) * HD].astype(jnp.float32) * q_cos
                + pltpu.roll(q_ref[:, head * HD : (head + 1) * HD].astype(jnp.float32), half_dim, 1) * q_sin
            ).astype(jnp.bfloat16)
            for head in range(group_size)
        ],
        axis=0,
    )
    scores = lax.dot_general(
        key_rot, stacked, (((1,), (1,)), ((), ())), preferred_element_type=jnp.float32
    )
    weights = []
    totals = []
    for head in range(group_size):
        part = scores[:, head * query_rows : (head + 1) * query_rows] * scale + bias
        largest = jnp.max(part, axis=0, keepdims=True)
        expw = jnp.exp(part - largest)
        totals.append(jnp.sum(expw, axis=0, keepdims=True))
        weights.append(expw.astype(jnp.bfloat16))
    numer = lax.dot_general(
        jnp.concatenate([far_ref[1], mid_ref[1], near_ref[1]], axis=0), jnp.concatenate(weights, axis=1), (((0,), (0,)), ((), ())),
        preferred_element_type=jnp.float32,
    )
    for head in range(group_size):
        cols = numer[:, head * query_rows : (head + 1) * query_rows] / totals[head]
        out_ref[0, :, head * HD : (head + 1) * HD] = cols.T.astype(jnp.bfloat16)


def attend_all(own_queries, far, mid, near, offsets, inverse, bias):
    angle = offsets[None] * inverse
    low = lax.broadcasted_iota(jnp.int32, angle.shape, 2) < HD // 2
    table = cos_and_sin(angle, low)
    cands = inverse.shape[0]
    key_rows = far.shape[1] + mid.shape[1] + near.shape[1]
    query_rows, width = own_queries.shape
    heads = width // HD
    flops = cands * heads * 4 * query_rows * key_rows * HD
    return pl.pallas_call(
        attention_kernel,
        out_shape=jax.ShapeDtypeStruct((cands, query_rows, width), jnp.bfloat16),
        grid=(cands,),
        in_specs=[
            pl.BlockSpec((query_rows, width), lambda c: (0, 0)),
            pl.BlockSpec(far.shape, lambda c: (0, 0, 0)),
            pl.BlockSpec(mid.shape, lambda c: (0, 0, 0)),
            pl.BlockSpec(near.shape, lambda c: (0, 0, 0)),
            pl.BlockSpec((1, key_rows, HD), lambda c: (c, 0, 0)),
            pl.BlockSpec(bias.T.shape, lambda c: (0, 0)),
        ],
        out_specs=pl.BlockSpec((1, query_rows, width), lambda c: (c, 0, 0)),
        cost_estimate=pl.CostEstimate(
            flops=flops,
            transcendentals=cands * heads * query_rows * key_rows,
            bytes_accessed=(far.size + mid.size + near.size) * 2 + own_queries.size * 2 + cands * query_rows * width * 2,
        ),
    )(own_queries, far, mid, near, table, bias.T)


def place_kernel(in_ref, out_ref):
    count, _, width = in_ref.shape
    for g in range(count):
        out_ref[:, g * width : (g + 1) * width] = in_ref[g]


def side_by_side(blocks):
    count, rows, width = blocks.shape
    step = count // 2
    return pl.pallas_call(
        place_kernel,
        out_shape=jax.ShapeDtypeStruct((rows, count * width), blocks.dtype),
        grid=(count // step,),
        in_specs=[pl.BlockSpec((step, rows, width), lambda g: (g, 0, 0))],
        out_specs=pl.BlockSpec((rows, step * width), lambda g: (0, g)),
    )(blocks)


def cyclic_shift(value, axis, steps):
    count = lax.axis_size(axis)
    return lax.ppermute(value, axis, [(source, (source + steps) % count) for source in range(count)])


def on_device(queries, keys_values, factors, lengths):
    row_count = queries.shape[0]
    group_width = queries.shape[1] // KVH
    device = lax.axis_index("doc")
    group = lax.axis_index("cand")
    query_index = device * row_count + jnp.arange(row_count, dtype=jnp.int32)
    key_index = (device - SPAN) * row_count + jnp.arange((SPAN + 1) * row_count, dtype=jnp.int32)
    far = passed_along(keys_values, "doc", SPAN)
    window = keys_values
    reach = 1
    while reach < SPAN:
        if 2 * reach == SPAN:
            mid = passed_along(window, "doc", reach)
            reach *= 2
            continue
        window = jnp.concatenate([passed_along(window, "doc", reach), window], axis=1)
        if reach == 1:
            window, factors, lengths, queries = lax.optimization_barrier(
                (window, factors, lengths, queries)
            )
        reach *= 2
    cands = lax.axis_size("cand")
    every_factor = lax.all_to_all(
        jnp.broadcast_to(factors, (cands, factors.shape[1])), "cand", 0, 0, tiled=True
    )
    query_doc, _ = locate(query_index, lengths)
    key_doc, key_offset = locate(key_index, lengths)
    allowed = (
        (key_doc[None, :] == query_doc[:, None])
        & (key_index[None, :] <= query_index[:, None])
        & (key_doc[None, :] >= 0)
    )
    bias = jnp.where(allowed, 0.0, -1e30).astype(jnp.float32)
    offsets = jnp.broadcast_to(key_offset.astype(jnp.float32)[:, None], (key_offset.shape[0], HD))
    own_queries = lax.dynamic_slice_in_dim(queries, group * group_width, group_width, 1)
    mixed = attend_all(own_queries, far, mid, window, offsets, inverse_rows(every_factor), bias)
    gathered = lax.all_to_all(mixed, "cand", 0, 0, tiled=True)
    return side_by_side(gathered)[None]


def solution(mesh):
    placed = (P("doc", None), P(None, "doc", "cand"), P("cand", None), P())
    return jax.shard_map(
        on_device, mesh=mesh, in_specs=placed, out_specs=P("cand", "doc", None), check_vma=False
    )
```

```python
import math

import jax
import jax.numpy as jnp
from jax import lax
from jax.experimental import pallas as pl
from jax.experimental.pallas import tpu as pltpu
from jax.sharding import PartitionSpec as P

H = 64
KVH = 8
HD = 128
SPAN = 8


ROPE_BASE = 500000.0


def passed_along(value, axis, steps):
    count = lax.axis_size(axis)
    first, last = (max(0, -steps), min(count, count - steps))
    return lax.ppermute(value, axis, [(source, source + steps) for source in range(first, last)])


def locate(index_rows, lengths):
    ends = jnp.cumsum(lengths)
    starts = ends - lengths
    docid = jnp.sum((index_rows[:, None] >= ends[None, :]).astype(jnp.int32), axis=1)
    onehot = docid[:, None] == jnp.arange(lengths.shape[0], dtype=jnp.int32)[None, :]
    first_row = jnp.sum(jnp.where(onehot, starts[None, :], 0), axis=1)
    valid = index_rows >= 0
    return (jnp.where(valid, docid, -1), jnp.where(valid, index_rows - first_row, 0))


def inverse_rows(factors):
    half_dim = HD // 2
    inverse = jnp.power(ROPE_BASE, -2.0 * jnp.arange(half_dim, dtype=jnp.float32) / HD) / factors
    return jnp.concatenate([inverse, inverse], axis=-1)[:, None, :]


def cos_and_sin(angle, low):
    turns = jnp.floor(angle * 0.636619772367581343 + 0.5)
    rest = ((angle - turns * 1.5703125) - turns * 4.837512969970703125e-4) - turns * 7.54978995489188216e-8
    square = rest * rest
    sine = rest + rest * square * (-1.6666654611e-1 + square * (8.3321608736e-3 + square * -1.9515295891e-4))
    cosine = 1.0 - 0.5 * square + square * square * (
        4.166664568298827e-2 + square * (-1.388731625493765e-3 + square * 2.443315711809948e-5)
    )
    quadrant = turns.astype(jnp.int32) + jnp.where(low, 0, 3)
    base = jnp.where((quadrant & 1) == 1, sine, cosine)
    return jnp.where(((quadrant + 1) & 2) != 0, -base, base)


def attention_kernel(q_ref, kv_ref, table_ref, bias_ref, out_ref):
    half_dim = HD // 2
    group_size = H // KVH
    query_rows = q_ref.shape[0]
    table = table_ref[0]
    low = lax.broadcasted_iota(jnp.int32, table.shape, 1) < half_dim
    swapped = pltpu.roll(table, half_dim, 1)
    cosine = jnp.where(low, table, swapped)
    sine = jnp.where(low, -swapped, table)
    keys = kv_ref[0].astype(jnp.float32)
    key_rot = (keys * cosine + pltpu.roll(keys, half_dim, 1) * sine).astype(jnp.bfloat16)
    first_query = table.shape[0] - query_rows
    q_cos = cosine[first_query:]
    q_sin = sine[first_query:]
    bias = bias_ref[...]
    scale = 1.0 / math.sqrt(HD)
    stacked = jnp.concatenate(
        [
            (
                q_ref[:, head * HD : (head + 1) * HD].astype(jnp.float32) * q_cos
                + pltpu.roll(q_ref[:, head * HD : (head + 1) * HD].astype(jnp.float32), half_dim, 1) * q_sin
            ).astype(jnp.bfloat16)
            for head in range(group_size)
        ],
        axis=0,
    )
    scores = lax.dot_general(
        key_rot, stacked, (((1,), (1,)), ((), ())), preferred_element_type=jnp.float32
    )
    weights = []
    totals = []
    for head in range(group_size):
        part = scores[:, head * query_rows : (head + 1) * query_rows] * scale + bias
        largest = jnp.max(part, axis=0, keepdims=True)
        expw = jnp.exp(part - largest)
        totals.append(jnp.sum(expw, axis=0, keepdims=True))
        weights.append(expw.astype(jnp.bfloat16))
    numer = lax.dot_general(
        kv_ref[1], jnp.concatenate(weights, axis=1), (((0,), (0,)), ((), ())),
        preferred_element_type=jnp.float32,
    )
    for head in range(group_size):
        cols = numer[:, head * query_rows : (head + 1) * query_rows] / totals[head]
        out_ref[0, :, head * HD : (head + 1) * HD] = cols.T.astype(jnp.bfloat16)


def attend_all(own_queries, window, offsets, inverse, bias):
    angle = offsets[None] * inverse
    low = lax.broadcasted_iota(jnp.int32, angle.shape, 2) < HD // 2
    table = cos_and_sin(angle, low)
    cands = inverse.shape[0]
    key_rows = window.shape[1]
    query_rows, width = own_queries.shape
    heads = width // HD
    flops = cands * heads * 4 * query_rows * key_rows * HD
    return pl.pallas_call(
        attention_kernel,
        out_shape=jax.ShapeDtypeStruct((cands, query_rows, width), jnp.bfloat16),
        grid=(cands,),
        in_specs=[
            pl.BlockSpec((query_rows, width), lambda c: (0, 0)),
            pl.BlockSpec(window.shape, lambda c: (0, 0, 0)),
            pl.BlockSpec((1, key_rows, HD), lambda c: (c, 0, 0)),
            pl.BlockSpec(bias.T.shape, lambda c: (0, 0)),
        ],
        out_specs=pl.BlockSpec((1, query_rows, width), lambda c: (c, 0, 0)),
        cost_estimate=pl.CostEstimate(
            flops=flops,
            transcendentals=cands * heads * query_rows * key_rows,
            bytes_accessed=window.size * 2 + own_queries.size * 2 + cands * query_rows * width * 2,
        ),
    )(own_queries, window, table, bias.T)


def place_kernel(in_ref, out_ref):
    count, _, width = in_ref.shape
    for g in range(count):
        out_ref[:, g * width : (g + 1) * width] = in_ref[g]


def side_by_side(blocks):
    count, rows, width = blocks.shape
    step = count // 4
    return pl.pallas_call(
        place_kernel,
        out_shape=jax.ShapeDtypeStruct((rows, count * width), blocks.dtype),
        grid=(count // step,),
        in_specs=[pl.BlockSpec((step, rows, width), lambda g: (g, 0, 0))],
        out_specs=pl.BlockSpec((rows, step * width), lambda g: (0, g)),
    )(blocks)


def cyclic_shift(value, axis, steps):
    count = lax.axis_size(axis)
    return lax.ppermute(value, axis, [(source, (source + steps) % count) for source in range(count)])


def on_device(queries, keys_values, factors, lengths):
    row_count = queries.shape[0]
    group_width = queries.shape[1] // KVH
    device = lax.axis_index("doc")
    group = lax.axis_index("cand")
    query_index = device * row_count + jnp.arange(row_count, dtype=jnp.int32)
    key_index = (device - SPAN) * row_count + jnp.arange((SPAN + 1) * row_count, dtype=jnp.int32)
    far = passed_along(keys_values, "doc", SPAN)
    window = keys_values
    reach = 1
    while reach < SPAN:
        window = jnp.concatenate([passed_along(window, "doc", reach), window], axis=1)
        if reach == 1:
            window, factors, lengths, queries = lax.optimization_barrier(
                (window, factors, lengths, queries)
            )
        reach *= 2
    window = jnp.concatenate([far, window], axis=1)
    cands = lax.axis_size("cand")
    every_factor = lax.all_to_all(
        jnp.broadcast_to(factors, (cands, factors.shape[1])), "cand", 0, 0, tiled=True
    )
    query_doc, _ = locate(query_index, lengths)
    key_doc, key_offset = locate(key_index, lengths)
    allowed = (
        (key_doc[None, :] == query_doc[:, None])
        & (key_index[None, :] <= query_index[:, None])
        & (key_doc[None, :] >= 0)
    )
    bias = jnp.where(allowed, 0.0, -1e30).astype(jnp.float32)
    offsets = jnp.broadcast_to(key_offset.astype(jnp.float32)[:, None], (key_offset.shape[0], HD))
    own_queries = lax.dynamic_slice_in_dim(queries, group * group_width, group_width, 1)
    mixed = attend_all(own_queries, window, offsets, inverse_rows(every_factor), bias)
    gathered = lax.all_to_all(mixed, "cand", 0, 0, tiled=True)
    return side_by_side(gathered)[None]


def solution(mesh):
    placed = (P("doc", None), P(None, "doc", "cand"), P("cand", None), P())
    return jax.shard_map(
        on_device, mesh=mesh, in_specs=placed, out_specs=P("cand", "doc", None), check_vma=False
    )
```

```python
import math

import jax
import jax.numpy as jnp
from jax import lax
from jax.experimental import pallas as pl
from jax.experimental.pallas import tpu as pltpu
from jax.sharding import PartitionSpec as P

H = 64
KVH = 8
HD = 128
SPAN = 8


ROPE_BASE = 500000.0


def passed_along(value, axis, steps):
    count = lax.axis_size(axis)
    first, last = (max(0, -steps), min(count, count - steps))
    return lax.ppermute(value, axis, [(source, source + steps) for source in range(first, last)])


def locate(index_rows, lengths):
    ends = jnp.cumsum(lengths)
    starts = ends - lengths
    docid = jnp.sum((index_rows[:, None] >= ends[None, :]).astype(jnp.int32), axis=1)
    onehot = docid[:, None] == jnp.arange(lengths.shape[0], dtype=jnp.int32)[None, :]
    first_row = jnp.sum(jnp.where(onehot, starts[None, :], 0), axis=1)
    valid = index_rows >= 0
    return (jnp.where(valid, docid, -1), jnp.where(valid, index_rows - first_row, 0))


def inverse_rows(factors):
    half_dim = HD // 2
    inverse = jnp.power(ROPE_BASE, -2.0 * jnp.arange(half_dim, dtype=jnp.float32) / HD) / factors
    return jnp.concatenate([inverse, inverse], axis=-1)[:, None, :]


def cos_and_sin(angle, low):
    turns = jnp.floor(angle * 0.636619772367581343 + 0.5)
    rest = ((angle - turns * 1.5703125) - turns * 4.837512969970703125e-4) - turns * 7.54978995489188216e-8
    square = rest * rest
    sine = rest + rest * square * (-1.6666654611e-1 + square * (8.3321608736e-3 + square * -1.9515295891e-4))
    cosine = 1.0 - 0.5 * square + square * square * (
        4.166664568298827e-2 + square * (-1.388731625493765e-3 + square * 2.443315711809948e-5)
    )
    quadrant = turns.astype(jnp.int32) + jnp.where(low, 0, 3)
    base = jnp.where((quadrant & 1) == 1, sine, cosine)
    return jnp.where(((quadrant + 1) & 2) != 0, -base, base)


def attention_kernel(q_ref, kv_ref, table_ref, bias_ref, out_ref):
    half_dim = HD // 2
    group_size = H // KVH
    query_rows = q_ref.shape[0]
    table = table_ref[0]
    low = lax.broadcasted_iota(jnp.int32, table.shape, 1) < half_dim
    swapped = pltpu.roll(table, half_dim, 1)
    cosine = jnp.where(low, table, swapped)
    sine = jnp.where(low, -swapped, table)
    keys = kv_ref[0].astype(jnp.float32)
    key_rot = (keys * cosine + pltpu.roll(keys, half_dim, 1) * sine).astype(jnp.bfloat16)
    first_query = table.shape[0] - query_rows
    q_cos = cosine[first_query:]
    q_sin = sine[first_query:]
    bias = bias_ref[...]
    scale = 1.0 / math.sqrt(HD)
    stacked = jnp.concatenate(
        [
            (
                q_ref[:, head * HD : (head + 1) * HD].astype(jnp.float32) * q_cos
                + pltpu.roll(q_ref[:, head * HD : (head + 1) * HD].astype(jnp.float32), half_dim, 1) * q_sin
            ).astype(jnp.bfloat16)
            for head in range(group_size)
        ],
        axis=0,
    )
    scores = lax.dot_general(
        key_rot, stacked, (((1,), (1,)), ((), ())), preferred_element_type=jnp.float32
    )
    weights = []
    totals = []
    for head in range(group_size):
        part = scores[:, head * query_rows : (head + 1) * query_rows] * scale + bias
        largest = jnp.max(part, axis=0, keepdims=True)
        expw = jnp.exp(part - largest)
        totals.append(jnp.sum(expw, axis=0, keepdims=True))
        weights.append(expw.astype(jnp.bfloat16))
    numer = lax.dot_general(
        kv_ref[1], jnp.concatenate(weights, axis=1), (((0,), (0,)), ((), ())),
        preferred_element_type=jnp.float32,
    )
    for head in range(group_size):
        cols = numer[:, head * query_rows : (head + 1) * query_rows] / totals[head]
        out_ref[0, :, head * HD : (head + 1) * HD] = cols.T.astype(jnp.bfloat16)


def attend_all(own_queries, window, offsets, inverse, bias):
    angle = offsets[None] * inverse
    low = lax.broadcasted_iota(jnp.int32, angle.shape, 2) < HD // 2
    table = cos_and_sin(angle, low)
    cands = inverse.shape[0]
    key_rows = window.shape[1]
    query_rows, width = own_queries.shape
    heads = width // HD
    flops = cands * heads * 4 * query_rows * key_rows * HD
    return pl.pallas_call(
        attention_kernel,
        out_shape=jax.ShapeDtypeStruct((cands, query_rows, width), jnp.bfloat16),
        grid=(cands,),
        in_specs=[
            pl.BlockSpec((query_rows, width), lambda c: (0, 0)),
            pl.BlockSpec(window.shape, lambda c: (0, 0, 0)),
            pl.BlockSpec((1, key_rows, HD), lambda c: (c, 0, 0)),
            pl.BlockSpec(bias.T.shape, lambda c: (0, 0)),
        ],
        out_specs=pl.BlockSpec((1, query_rows, width), lambda c: (c, 0, 0)),
        cost_estimate=pl.CostEstimate(
            flops=flops,
            transcendentals=cands * heads * query_rows * key_rows,
            bytes_accessed=window.size * 2 + own_queries.size * 2 + cands * query_rows * width * 2,
        ),
    )(own_queries, window, table, bias.T)


def place_kernel(in_ref, out_ref):
    count, _, width = in_ref.shape
    for g in range(count):
        out_ref[:, g * width : (g + 1) * width] = in_ref[g]


def side_by_side(blocks):
    count, rows, width = blocks.shape
    step = count
    return pl.pallas_call(
        place_kernel,
        out_shape=jax.ShapeDtypeStruct((rows, count * width), blocks.dtype),
        grid=(count // step,),
        in_specs=[pl.BlockSpec((step, rows, width), lambda g: (g, 0, 0))],
        out_specs=pl.BlockSpec((rows, step * width), lambda g: (0, g)),
    )(blocks)


def cyclic_shift(value, axis, steps):
    count = lax.axis_size(axis)
    return lax.ppermute(value, axis, [(source, (source + steps) % count) for source in range(count)])


def on_device(queries, keys_values, factors, lengths):
    row_count = queries.shape[0]
    group_width = queries.shape[1] // KVH
    device = lax.axis_index("doc")
    group = lax.axis_index("cand")
    query_index = device * row_count + jnp.arange(row_count, dtype=jnp.int32)
    key_index = (device - SPAN) * row_count + jnp.arange((SPAN + 1) * row_count, dtype=jnp.int32)
    far = passed_along(keys_values, "doc", SPAN)
    window = keys_values
    reach = 1
    while reach < SPAN:
        window = jnp.concatenate([passed_along(window, "doc", reach), window], axis=1)
        if reach == 1:
            window, factors, lengths, queries = lax.optimization_barrier(
                (window, factors, lengths, queries)
            )
        reach *= 2
    window = jnp.concatenate([far, window], axis=1)
    cands = lax.axis_size("cand")
    every_factor = lax.all_to_all(
        jnp.broadcast_to(factors, (cands, factors.shape[1])), "cand", 0, 0, tiled=True
    )
    query_doc, _ = locate(query_index, lengths)
    key_doc, key_offset = locate(key_index, lengths)
    allowed = (
        (key_doc[None, :] == query_doc[:, None])
        & (key_index[None, :] <= query_index[:, None])
        & (key_doc[None, :] >= 0)
    )
    bias = jnp.where(allowed, 0.0, -1e30).astype(jnp.float32)
    offsets = jnp.broadcast_to(key_offset.astype(jnp.float32)[:, None], (key_offset.shape[0], HD))
    own_queries = lax.dynamic_slice_in_dim(queries, group * group_width, group_width, 1)
    mixed = attend_all(own_queries, window, offsets, inverse_rows(every_factor), bias)
    gathered = lax.all_to_all(mixed, "cand", 0, 0, tiled=True)
    return side_by_side(gathered)[None]


def solution(mesh):
    placed = (P("doc", None), P(None, "doc", "cand"), P("cand", None), P())
    return jax.shard_map(
        on_device, mesh=mesh, in_specs=placed, out_specs=P("cand", "doc", None), check_vma=False
    )
```
